128 devices in a mesh: gz: 16 (over z, x), gx: 8 (over y, core).
Axes of the slice: x: 4, y: 4, z: 4, core: 2. Of those that a mesh axis runs over, the one named last changes fastest.
Arguments:
- rhs_temp: float32 [1024, 128, 128], P('gz', 'gx'), may hold values from -24 to 24
- rhs_ion: float32 [1024, 128, 128], P('gz', 'gx'), may hold values from -24 to 24
- cond_temp: float32 [1024, 128, 128], P('gz', 'gx'), may hold values from 20000 to 300000
- cond_ion: float32 [1024, 128, 128], P('gz', 'gx'), may hold values from 20000 to 300000
- bubble_target: int32 [16, 2048], P('gz', 'gx'), may hold values from 0 to 8191, as said below
- bubble_sink: float32 [16, 2048, 128], P('gz', 'gx'), may hold values from 2 to 20
- bubble_void: float32 [16, 2048, 128], P('gz', 'gx'), may hold values from 0.05 to 0.5
Outputs:
- temp_new: float32 [1024, 128, 128], P('gz', 'gx')
- ion_new: float32 [1024, 128, 128], P('gz', 'gx')
The draws below stay inside these ranges and needn't reach their ends.
Inputs may be any that keep to these rules, and one draw needn't show every extreme that they name: `bubble_target`: in every draw one index of gx receives exactly 96 blocks from every device of each gz index; no device sends more than 96 blocks to one index of gx; the other indices of gx receive a device's remaining blocks in nearly equal numbers; cells within a device are independent and may repeat.
All inputs are finite; a program needn't handle non-finite values.
Results may differ from the reference program's by a relative error of at most 0.0007.
Values sent between devices are 32-bit elements; how exact they have to be, the bound alone decides.
No kernel may reach another device: no remote copies, remote signals or barrier semaphores. Data moves between devices by JAX's collectives and lax.ppermute only.
A program may use at most 64 MiB of HBM per device.

```python
import math
import jax
import jax.numpy as jnp
from jax import lax

CZ = 64
CX = 16
NY = 128
NB_DEV = 256
NZ = 1024
NX = 128
CAP = 96
N_GZ = 16
N_GX = 8


def field_draw(key, salt):
    field_key = jax.random.fold_in(key, salt)
    shape = (NZ, NX, NY)
    values = jnp.clip(2.0 + 6.0 * jax.random.normal(field_key, shape, jnp.float32), -24.0, 24.0)
    return values


def draw_rhs_temp(key, part):
    return field_draw(key, 5)


def draw_rhs_ion(key, part):
    return field_draw(key, 7)


def draw_bubble_target(key, part):
    cell_total = CZ * CX
    hot_key, order_key, cell_key = jax.random.split(jax.random.fold_in(key, 23), 3)
    hottest = jax.random.randint(hot_key, (), 0, N_GX).astype(jnp.int32)
    slot_ids = jnp.arange(NB_DEV, dtype=jnp.int32)
    others = (slot_ids - CAP) % (N_GX - 1)
    others = others + (others >= hottest).astype(jnp.int32)
    base_owner = jnp.where(slot_ids < CAP, hottest, others)
    device_keys = jax.random.split(order_key, N_GZ * N_GX)
    orders = jax.vmap(lambda one_key: jax.random.permutation(one_key, NB_DEV))(device_keys)
    owners = base_owner[orders]
    cell_ids = jax.random.randint(cell_key, (N_GZ * N_GX, NB_DEV), 0, cell_total).astype(jnp.int32)
    high_slot = jnp.argmax((owners[0] == N_GX - 1).astype(jnp.int32))
    low_slot = jnp.argmax((owners[0] == 0).astype(jnp.int32))
    cell_ids = cell_ids.at[0, high_slot].set(cell_total - 1)
    cell_ids = cell_ids.at[0, low_slot].set(0)
    return (owners * cell_total + cell_ids).reshape(N_GZ, N_GX * NB_DEV).astype(jnp.int32)


def steps_of(own_key, shape, cuts, least, top_value):
    def one(position, parts):
        draws = jax.random.uniform(jax.random.fold_in(jax.random.fold_in(own_key, 6), position), (parts,), jnp.float32, least / len(cuts), top_value / len(cuts))
        return jnp.repeat(jnp.exp(draws), shape[position] // parts).reshape((-1,) + (1,) * (len(shape) - position - 1))

    loudness = one(*cuts[0])
    for cut in cuts[1:]:
        loudness = loudness * one(*cut)
    return loudness


def setup_inputs(seed: int = 0) -> dict:
    seeds = jax.random.split(jax.random.key(seed), 8)
    rhs_temp = draw_rhs_temp(jax.random.fold_in(seeds[7], 71), 0)
    rhs_ion = draw_rhs_ion(jax.random.fold_in(seeds[7], 71), 0)
    cond_temp = jnp.clip(jnp.exp(math.log(300000.0) - 2.7080502 * jax.random.uniform(seeds[2], (NZ, NX, NY), jnp.float32) ** steps_of(seeds[2], (NZ, NX, NY), ((0, 16), (1, 8)), -0.2, 0.2)), 20000.0, 300000.0)
    cond_ion = jnp.clip(jnp.exp(math.log(300000.0) - 2.7080502 * jax.random.uniform(seeds[3], (NZ, NX, NY), jnp.float32) ** steps_of(seeds[3], (NZ, NX, NY), ((0, 16), (1, 8)), -0.2, 0.2)), 20000.0, 300000.0)
    bubble_target = draw_bubble_target(jax.random.fold_in(seeds[7], 71), 0)
    bubble_sink = jnp.clip(jnp.exp(math.log(20.0) - 2.3025851 * jax.random.uniform(seeds[5], (N_GZ, N_GX * NB_DEV, NY), jnp.float32) ** steps_of(seeds[5], (N_GZ, N_GX * NB_DEV, NY), ((0, 16), (1, 8)), -0.2, 0.2)), 2.0, 20.0)
    bubble_void = jnp.clip(0.05 + 0.45 * jax.random.uniform(seeds[6], (N_GZ, N_GX * NB_DEV, NY), jnp.float32) ** steps_of(seeds[6], (N_GZ, N_GX * NB_DEV, NY), ((0, 16), (1, 8)), -0.2, 0.2), 0.05, 0.5)
    return {"rhs_temp": rhs_temp, "rhs_ion": rhs_ion, "cond_temp": cond_temp, "cond_ion": cond_ion, "bubble_target": bubble_target, "bubble_sink": bubble_sink, "bubble_void": bubble_void}


ion_rate = 40.0


def face_values(conductance):
    inner = 2.0 * conductance[:-1] * conductance[1:] / (conductance[:-1] + conductance[1:])
    below = jnp.concatenate([2.0 * conductance[:1], inner], axis=0)
    above = jnp.concatenate([inner, jnp.zeros_like(conductance[:1])], axis=0)
    return below, above


def deposit(bubble_target, payload):
    cell_total = CZ * CX
    owner_index = bubble_target // cell_total
    within = bubble_target % cell_total
    chain_index = jnp.arange(N_GZ, dtype=jnp.int32)[:, None]
    z_index = (chain_index * CZ + within // CX).astype(jnp.int32)
    x_index = (owner_index * CX + within % CX).astype(jnp.int32)
    return jnp.zeros((NZ, NX, NY), jnp.float32).at[z_index, x_index].add(payload)


def thomas_solve(lower_band, main_band, upper_band, rights):
    def forward(carry, entries):
        factor_prev, value_prev = carry
        low_row, main_row, up_row, right_row = entries
        pivot_value = main_row - low_row * factor_prev
        factor_next = up_row / pivot_value
        value_next = (right_row - low_row * value_prev) / pivot_value
        return (factor_next, value_next), (factor_next, value_next)

    start = jnp.zeros(rights.shape[1:], jnp.float32)
    _, (factors, values) = lax.scan(forward, (start, start), (lower_band, main_band, upper_band, rights))

    def backward(next_value, entries):
        factor_row, value_row = entries
        solved = value_row - factor_row * next_value
        return solved, solved

    _, solution = lax.scan(backward, start, (factors, values), reverse=True)
    return solution


def implicit_step(rights, conductance, absorb):
    below, above = face_values(conductance)
    return thomas_solve(-below, 1.0 + below + above + absorb, -above, rights)


def reference(rhs_temp, rhs_ion, cond_temp, cond_ion, bubble_target, bubble_sink, bubble_void):
    sink = deposit(bubble_target, bubble_sink)
    void = deposit(bubble_target, bubble_void)
    temp_new = implicit_step(rhs_temp, cond_temp, sink)
    ion_new = implicit_step(rhs_ion, cond_ion, ion_rate * void)
    return temp_new, ion_new
```

```python
import functools

import jax
import jax.numpy as jnp
from jax import lax
from jax.experimental import pallas as pl
from jax.experimental.pallas import tpu as pltpu
from jax.sharding import PartitionSpec as P

ion_rate = 40.0
HIGHEST = lax.Precision.HIGHEST


def face(lower, upper):
    return 2.0 * lower * upper / (lower + upper)


def local_kernel(rt_ref, ri_ref, ct_ref, ci_ref, src_ref, lo_ref, hi_ref,
                 yt_ref, yi_ref, vt_ref, vi_ref, wt_ref, wi_ref):
    z_cells = rt_ref.shape[0]
    y_cells = rt_ref.shape[2]
    fields = (
        (rt_ref, ct_ref, yt_ref, vt_ref, wt_ref, 0, 1.0),
        (ri_ref, ci_ref, yi_ref, vi_ref, wi_ref, 1, ion_rate),
    )

    def absorb_of(k, z):
        part = src_ref[z, :, k * y_cells:(k + 1) * y_cells]
        return part if k == 0 else ion_rate * part

    carry = []
    for rhs_ref, c_ref, y_ref, v_ref, w_ref, k, _ in fields:
        below = lo_ref[k]
        above = face(c_ref[0], c_ref[1])
        main = 1.0 + below + above + absorb_of(k, 0)
        rp = 1.0 / main
        f = -above * rp
        dy = rhs_ref[0] * rp
        dv = rp
        w_ref[0] = f
        y_ref[0] = dy
        v_ref[0] = dv
        carry += [above, f, dy, dv]

    def fwd(z, carry):
        out = []
        for n, (rhs_ref, c_ref, y_ref, v_ref, w_ref, k, _) in enumerate(fields):
            below, f_prev, dy_prev, dv_prev = carry[4 * n:4 * n + 4]
            above = face(c_ref[z], c_ref[z + 1])
            main = 1.0 + below + above + absorb_of(k, z)
            pivot = main + below * f_prev
            rp = 1.0 / pivot
            f = -above * rp
            dy = (rhs_ref[z] + below * dy_prev) * rp
            dv = (below * dv_prev) * rp
            w_ref[z] = f
            y_ref[z] = dy
            v_ref[z] = dv
            out += [above, f, dy, dv]
        return tuple(out)

    carry = lax.fori_loop(1, z_cells - 1, fwd, tuple(carry), unroll=2)

    z = z_cells - 1
    back = []
    for n, (rhs_ref, c_ref, y_ref, v_ref, w_ref, k, _) in enumerate(fields):
        below, f_prev, dy_prev, dv_prev = carry[4 * n:4 * n + 4]
        above = hi_ref[k]
        main = 1.0 + below + above + absorb_of(k, z)
        pivot = main + below * f_prev
        rp = 1.0 / pivot
        dy = (rhs_ref[z] + below * dy_prev) * rp
        dv = (below * dv_prev) * rp
        y_ref[z] = dy
        v_ref[z] = dv
        w_ref[z] = rp
        back += [dy, dv, rp]

    def bwd(i, back):
        z = z_cells - 2 - i
        out = []
        for n, (rhs_ref, c_ref, y_ref, v_ref, w_ref, k, _) in enumerate(fields):
            y_next, v_next, w_next = back[3 * n:3 * n + 3]
            f = w_ref[z]
            y_val = y_ref[z] - f * y_next
            v_val = v_ref[z] - f * v_next
            w_val = -f * w_next
            y_ref[z] = y_val
            v_ref[z] = v_val
            w_ref[z] = w_val
            out += [y_val, v_val, w_val]
        return tuple(out)

    lax.fori_loop(0, z_cells - 1, bwd, tuple(back), unroll=2)


def local_solve(rhs_temp, rhs_ion, cond_temp, cond_ion, sources, lo, hi):
    shape = jax.ShapeDtypeStruct(rhs_temp.shape, jnp.float32)
    vmem = pl.BlockSpec(memory_space=pltpu.VMEM)
    return pl.pallas_call(
        local_kernel,
        out_shape=(shape,) * 6,
        in_specs=[vmem] * 7,
        out_specs=(vmem,) * 6,
    )(rhs_temp, rhs_ion, cond_temp, cond_ion, sources, lo, hi)


def deposit(bubble_target, bubble_sink, bubble_void, z_cells, x_cells, y_cells):
    cell_total = z_cells * x_cells
    groups = lax.axis_size("gx")
    target = bubble_target[0]
    record_total = target.shape[0]
    slot_count = 3 * record_total // groups
    width = 2 * y_cells
    payload = jnp.concatenate([bubble_sink[0], bubble_void[0]], axis=1)
    destination = target // cell_total
    cell_index = target % cell_total
    same_owner = destination[:, None] == destination[None, :]
    row_ids = lax.broadcasted_iota(jnp.int32, (record_total, record_total), 0)
    col_ids = lax.broadcasted_iota(jnp.int32, (record_total, record_total), 1)
    rank_within = jnp.sum((same_owner & (row_ids > col_ids)).astype(jnp.int32), axis=1)
    slot_index = destination * slot_count + rank_within
    slot_ids = lax.broadcasted_iota(jnp.int32, (groups * slot_count, record_total), 0)
    pick = slot_ids == slot_index[None, :]
    send_rows = jnp.dot(pick.astype(jnp.float32), payload, precision=HIGHEST)
    cell_plus = (cell_index + 1).astype(jnp.float32)
    send_cells = jnp.sum(jnp.where(pick, cell_plus[None, :], 0.0), axis=1) - 1.0
    cell_row = jnp.pad(send_cells.reshape(groups, 1, slot_count), ((0, 0), (0, 0), (0, width - slot_count)))
    send = jnp.concatenate([send_rows.reshape(groups, slot_count, width), cell_row], axis=1)
    received = lax.all_to_all(send, "gx", split_axis=0, concat_axis=0, tiled=True)
    rows = received[:, :slot_count, :].reshape(groups * slot_count, width)
    cells = received[:, slot_count, :slot_count].reshape(groups * slot_count)
    cell_ids = lax.broadcasted_iota(jnp.int32, (cell_total, groups * slot_count), 0).astype(jnp.float32)
    spread = (cell_ids == cells[None, :]).astype(jnp.float32)
    sources = jnp.dot(spread, rows, precision=HIGHEST)
    return sources.reshape(z_cells, x_cells, width)


def body(rhs_temp, rhs_ion, cond_temp, cond_ion, bubble_target, bubble_sink, bubble_void):
    z_cells, x_cells, y_cells = rhs_temp.shape
    chain = lax.axis_size("gz")
    position = lax.axis_index("gz")
    sources = deposit(bubble_target, bubble_sink, bubble_void, z_cells, x_cells, y_cells)

    first = jnp.stack([cond_temp[0], cond_ion[0]])
    last = jnp.stack([cond_temp[-1], cond_ion[-1]])
    from_below = lax.ppermute(last, "gz", [(i, i + 1) for i in range(chain - 1)])
    from_above = lax.ppermute(first, "gz", [(i + 1, i) for i in range(chain - 1)])
    lo = jnp.where(position == 0, 2.0 * first, face(from_below, first))
    hi = jnp.where(position == chain - 1, 0.0, face(last, from_above))

    yt, yi, vt, vi, wt, wi = local_solve(rhs_temp, rhs_ion, cond_temp, cond_ion, sources, lo, hi)
    y = (yt, yi)
    v = (vt, vi)
    w = (wt, wi)
    beta = jnp.where(position == 0, 0.0, lo)
    alpha = hi
    pack = []
    for k in range(2):
        pack += [
            -v[k][0] * beta[k],
            -w[k][0] * alpha[k],
            -v[k][-1] * beta[k],
            -w[k][-1] * alpha[k],
            y[k][0],
            y[k][-1],
        ]
    gathered = lax.all_gather(jnp.stack(pack), "gz")

    outs = []
    for k in range(2):
        a, b, c, e, yf, yl = (gathered[:, 6 * k + m] for m in range(6))
        g1_prev = jnp.zeros_like(a[0])
        zl_prev = jnp.zeros_like(a[0])
        g0s, z0s, g1s, zls = [], [], [], []
        for d in range(chain):
            p = 1.0 - a[d] * g1_prev
            g0 = b[d] / p
            z0 = (yf[d] - a[d] * zl_prev) / p
            t = c[d] * g1_prev
            g1 = e[d] + t * g0
            zl = yl[d] - c[d] * zl_prev + t * z0
            g0s.append(g0)
            z0s.append(z0)
            g1s.append(g1)
            zls.append(zl)
            g1_prev, zl_prev = g1, zl
        f_next = jnp.zeros_like(a[0])
        firsts = [None] * chain
        lasts = [None] * chain
        for d in reversed(range(chain)):
            firsts[d] = z0s[d] - g0s[d] * f_next
            lasts[d] = zls[d] - g1s[d] * f_next
            f_next = firsts[d]
        zero = jnp.zeros_like(a[0])
        last_prev = jnp.stack([zero] + lasts[:-1])[position]
        first_next = jnp.stack(firsts[1:] + [zero])[position]
        outs.append(
            y[k]
            + v[k] * (beta[k] * last_prev)[None]
            + w[k] * (alpha[k] * first_next)[None]
        )
    return tuple(outs)


def solution(mesh):
    in_specs = (
        P("gz", "gx", None),
        P("gz", "gx", None),
        P("gz", "gx", None),
        P("gz", "gx", None),
        P("gz", "gx"),
        P("gz", "gx", None),
        P("gz", "gx", None),
    )
    out_specs = (P("gz", "gx", None), P("gz", "gx", None))
    return jax.shard_map(body, mesh=mesh, in_specs=in_specs, out_specs=out_specs, check_vma=False)
```

```python
import functools

import jax
import jax.numpy as jnp
from jax import lax
from jax.experimental import pallas as pl
from jax.experimental.pallas import tpu as pltpu
from jax.sharding import PartitionSpec as P

ion_rate = 40.0
HIGHEST = lax.Precision.HIGHEST


def face(lower, upper):
    return 2.0 * lower * upper / (lower + upper)


def local_kernel(rt_ref, ri_ref, ct_ref, ci_ref, src_ref, lo_ref, hi_ref, beta_ref,
                 yt_ref, yi_ref, vt_ref, vi_ref, wt_ref, wi_ref, pack_ref):
    z_cells = rt_ref.shape[0]
    y_cells = rt_ref.shape[2]
    fields = (
        (rt_ref, ct_ref, yt_ref, vt_ref, wt_ref, 0, 1.0),
        (ri_ref, ci_ref, yi_ref, vi_ref, wi_ref, 1, ion_rate),
    )

    def absorb_of(k, z):
        part = src_ref[z, :, k * y_cells:(k + 1) * y_cells]
        return part if k == 0 else ion_rate * part

    carry = []
    for rhs_ref, c_ref, y_ref, v_ref, w_ref, k, _ in fields:
        below = lo_ref[k]
        above = face(c_ref[0], c_ref[1])
        main = 1.0 + below + above + absorb_of(k, 0)
        rp = 1.0 / main
        f = -above * rp
        dy = rhs_ref[0] * rp
        dv = rp
        w_ref[0] = f
        y_ref[0] = dy
        v_ref[0] = dv
        carry += [above, f, dy, dv]

    def fwd(z, carry):
        out = []
        for n, (rhs_ref, c_ref, y_ref, v_ref, w_ref, k, _) in enumerate(fields):
            below, f_prev, dy_prev, dv_prev = carry[4 * n:4 * n + 4]
            above = face(c_ref[z], c_ref[z + 1])
            main = 1.0 + below + above + absorb_of(k, z)
            pivot = main + below * f_prev
            rp = 1.0 / pivot
            f = -above * rp
            dy = (rhs_ref[z] + below * dy_prev) * rp
            dv = (below * dv_prev) * rp
            w_ref[z] = f
            y_ref[z] = dy
            v_ref[z] = dv
            out += [above, f, dy, dv]
        return tuple(out)

    carry = lax.fori_loop(1, z_cells - 1, fwd, tuple(carry), unroll=2)

    z = z_cells - 1
    back = []
    for n, (rhs_ref, c_ref, y_ref, v_ref, w_ref, k, _) in enumerate(fields):
        below, f_prev, dy_prev, dv_prev = carry[4 * n:4 * n + 4]
        above = hi_ref[k]
        main = 1.0 + below + above + absorb_of(k, z)
        pivot = main + below * f_prev
        rp = 1.0 / pivot
        dy = (rhs_ref[z] + below * dy_prev) * rp
        dv = (below * dv_prev) * rp
        y_ref[z] = dy
        v_ref[z] = dv
        w_ref[z] = rp
        back += [dy, dv, rp]

    def bwd(i, back):
        z = z_cells - 2 - i
        out = []
        for n, (rhs_ref, c_ref, y_ref, v_ref, w_ref, k, _) in enumerate(fields):
            y_next, v_next, w_next = back[3 * n:3 * n + 3]
            f = w_ref[z]
            y_val = y_ref[z] - f * y_next
            v_val = v_ref[z] - f * v_next
            w_val = -f * w_next
            y_ref[z] = y_val
            v_ref[z] = v_val
            w_ref[z] = w_val
            out += [y_val, v_val, w_val]
        return tuple(out)

    back = lax.fori_loop(0, z_cells - 1, bwd, tuple(back), unroll=2)
    for n, (rhs_ref, c_ref, y_ref, v_ref, w_ref, k, _) in enumerate(fields):
        y_first, v_first, w_first = back[3 * n:3 * n + 3]
        beta = beta_ref[k]
        alpha = hi_ref[k]
        pack_ref[0, k] = -v_first * beta
        pack_ref[1, k] = -w_first * alpha
        pack_ref[2, k] = -v_ref[z_cells - 1] * beta
        pack_ref[3, k] = -w_ref[z_cells - 1] * alpha
        pack_ref[4, k] = y_first
        pack_ref[5, k] = y_ref[z_cells - 1]


def local_solve(rhs_temp, rhs_ion, cond_temp, cond_ion, sources, lo, hi, beta):
    shape = jax.ShapeDtypeStruct(rhs_temp.shape, jnp.float32)
    pack = jax.ShapeDtypeStruct((6,) + lo.shape, jnp.float32)
    vmem = pl.BlockSpec(memory_space=pltpu.VMEM)
    return pl.pallas_call(
        local_kernel,
        out_shape=(shape,) * 6 + (pack,),
        in_specs=[vmem] * 8,
        out_specs=(vmem,) * 7,
    )(rhs_temp, rhs_ion, cond_temp, cond_ion, sources, lo, hi, beta)


def chain_solve(packs, rights):
    count = len(packs)
    g1_prev = None
    zl_prev = None
    steps = []
    for i in range(count):
        a, b, c, e = packs[i]
        if g1_prev is None:
            z0 = [yf for yf, yl in rights[i]]
            zl = [yl for yf, yl in rights[i]]
            g0 = b
            g1 = e
        else:
            p = 1.0 - a * g1_prev
            rp = 1.0 / p
            g0 = b * rp
            t = c * g1_prev
            g1 = e + t * g0
            z0 = [(yf - a * zp) * rp for (yf, yl), zp in zip(rights[i], zl_prev)]
            zl = [yl - c * zp + t * z for (yf, yl), zp, z in zip(rights[i], zl_prev, z0)]
        steps.append((g0, g1, z0, zl))
        g1_prev, zl_prev = g1, zl
    firsts = [None] * count
    lasts = [None] * count
    f_next = None
    for i in reversed(range(count)):
        g0, g1, z0, zl = steps[i]
        if f_next is None:
            firsts[i], lasts[i] = z0, zl
        else:
            firsts[i] = [z - g0 * f for z, f in zip(z0, f_next)]
            lasts[i] = [z - g1 * f for z, f in zip(zl, f_next)]
        f_next = firsts[i]
    return firsts, lasts


def gather_ring(pack, size, stride, index):
    chain = lax.axis_size("gz")
    got = {0: pack}
    for s in range(1, size):
        route = []
        for i in range(chain):
            base = i - (i // stride % size) * stride
            route.append((i, base + ((i // stride + s) % size) * stride))
        got[s] = lax.ppermute(pack, "gz", route)
    ordered = []
    for member in range(size):
        pick = got[0]
        for s in range(1, size):
            pick = jnp.where((index - member) % size == s, got[s], pick)
        ordered.append(pick)
    return ordered


def select(values, index):
    out = jnp.zeros_like(values[0])
    for i, value in enumerate(values):
        out = jnp.where(index == i, value, out)
    return out


def deposit(bubble_target, bubble_sink, bubble_void, z_cells, x_cells, y_cells):
    cell_total = z_cells * x_cells
    groups = lax.axis_size("gx")
    target = bubble_target[0]
    record_total = target.shape[0]
    slot_count = 3 * record_total // groups
    width = 2 * y_cells
    payload = jnp.concatenate([bubble_sink[0], bubble_void[0]], axis=1)
    destination = target // cell_total
    cell_index = target % cell_total
    same_owner = destination[:, None] == destination[None, :]
    row_ids = lax.broadcasted_iota(jnp.int32, (record_total, record_total), 0)
    col_ids = lax.broadcasted_iota(jnp.int32, (record_total, record_total), 1)
    rank_within = jnp.sum((same_owner & (row_ids > col_ids)).astype(jnp.int32), axis=1)
    slot_index = destination * slot_count + rank_within
    slot_ids = lax.broadcasted_iota(jnp.int32, (groups * slot_count, record_total), 0)
    pick = slot_ids == slot_index[None, :]
    send_rows = jnp.dot(pick.astype(jnp.float32), payload, precision=HIGHEST)
    cell_plus = (cell_index + 1).astype(jnp.float32)
    send_cells = jnp.sum(jnp.where(pick, cell_plus[None, :], 0.0), axis=1) - 1.0
    cell_row = jnp.pad(send_cells.reshape(groups, 1, slot_count), ((0, 0), (0, 0), (0, width - slot_count)))
    send = jnp.concatenate([send_rows.reshape(groups, slot_count, width), cell_row], axis=1)
    received = lax.all_to_all(send, "gx", split_axis=0, concat_axis=0, tiled=True)
    rows = received[:, :slot_count, :].reshape(groups * slot_count, width)
    cells = received[:, slot_count, :slot_count].reshape(groups * slot_count)
    cell_ids = lax.broadcasted_iota(jnp.int32, (cell_total, groups * slot_count), 0).astype(jnp.float32)
    spread = (cell_ids == cells[None, :]).astype(jnp.float32)
    sources = jnp.dot(spread, rows, precision=HIGHEST)
    return sources.reshape(z_cells, x_cells, width)


def body(rhs_temp, rhs_ion, cond_temp, cond_ion, bubble_target, bubble_sink, bubble_void):
    z_cells, x_cells, y_cells = rhs_temp.shape
    chain = lax.axis_size("gz")
    position = lax.axis_index("gz")
    sources = deposit(bubble_target, bubble_sink, bubble_void, z_cells, x_cells, y_cells)

    first = jnp.stack([cond_temp[0], cond_ion[0]])
    last = jnp.stack([cond_temp[-1], cond_ion[-1]])
    from_below = lax.ppermute(last, "gz", [(i, i + 1) for i in range(chain - 1)])
    from_above = lax.ppermute(first, "gz", [(i + 1, i) for i in range(chain - 1)])
    lo = jnp.where(position == 0, 2.0 * first, face(from_below, first))
    hi = jnp.where(position == chain - 1, 0.0, face(last, from_above))

    beta = jnp.where(position == 0, 0.0, lo)
    alpha = hi
    yt, yi, vt, vi, wt, wi, pack = local_solve(
        rhs_temp, rhs_ion, cond_temp, cond_ion, sources, lo, hi, beta
    )
    size = 4 if chain % 4 == 0 and chain > 4 else chain
    groups_z = chain // size
    member = position % size
    group = position // size
    zero = jnp.zeros_like(lo)

    members = gather_ring(pack, size, 1, member)
    packs, rights = [], []
    for r, m in enumerate(members):
        a, b, c, e, yf, yl = (m[j] for j in range(6))
        right_sets = [(yf, yl), (zero, zero), (zero, zero)]
        if r == 0:
            right_sets[1] = (-a, -c)
            a, c = zero, zero
        if r == size - 1:
            right_sets[2] = (-b, -e)
            b, e = zero, zero
        packs.append((a, b, c, e))
        rights.append(right_sets)
    firsts, lasts = chain_solve(packs, rights)
    if groups_z > 1:
        group_pack = jnp.stack([
            -firsts[0][1], -firsts[0][2], -lasts[-1][1], -lasts[-1][2], firsts[0][0], lasts[-1][0]
        ])
        tops = gather_ring(group_pack, groups_z, size, group)
        gpacks = [(t[0], t[1], t[2], t[3]) for t in tops]
        grights = [[(t[4], t[5])] for t in tops]
        gfirsts, glasts = chain_solve(gpacks, grights)
        outside_low = select([zero] + [l[0] for l in glasts[:-1]], group)
        outside_high = select([f[0] for f in gfirsts[1:]] + [zero], group)
    else:
        outside_low = zero
        outside_high = zero

    def value(parts):
        return parts[0] + outside_low * parts[1] + outside_high * parts[2]

    last_prev = select([outside_low] + [value(l) for l in lasts[:-1]], member)
    first_next = select([value(f) for f in firsts[1:]] + [outside_high], member)
    y = (yt, yi)
    v = (vt, vi)
    w = (wt, wi)
    outs = []
    for k in range(2):
        outs.append(
            y[k]
            + v[k] * (beta[k] * last_prev[k])[None]
            + w[k] * (alpha[k] * first_next[k])[None]
        )
    return tuple(outs)


def solution(mesh):
    in_specs = (
        P("gz", "gx", None),
        P("gz", "gx", None),
        P("gz", "gx", None),
        P("gz", "gx", None),
        P("gz", "gx"),
        P("gz", "gx", None),
        P("gz", "gx", None),
    )
    out_specs = (P("gz", "gx", None), P("gz", "gx", None))
    return jax.shard_map(body, mesh=mesh, in_specs=in_specs, out_specs=out_specs, check_vma=False)
```

```python
import functools

import jax
import jax.numpy as jnp
from jax import lax
from jax.experimental import pallas as pl
from jax.experimental.pallas import tpu as pltpu
from jax.sharding import PartitionSpec as P

ion_rate = 40.0
HIGH = lax.Precision.HIGH


def face(lower, upper):
    return 2.0 * lower * upper / (lower + upper)


def local_kernel(rt_ref, ri_ref, ct_ref, ci_ref, src_ref, lo_ref, hi_ref, beta_ref,
                 yt_ref, yi_ref, vt_ref, vi_ref, wt_ref, wi_ref, pack_ref):
    z_cells = rt_ref.shape[0]
    y_cells = rt_ref.shape[2]
    fields = (
        (rt_ref, ct_ref, yt_ref, vt_ref, wt_ref, 0, 1.0),
        (ri_ref, ci_ref, yi_ref, vi_ref, wi_ref, 1, ion_rate),
    )

    def absorb_of(k, z):
        part = src_ref[z, :, k * y_cells:(k + 1) * y_cells]
        return part if k == 0 else ion_rate * part

    carry = []
    for rhs_ref, c_ref, y_ref, v_ref, w_ref, k, _ in fields:
        below = lo_ref[k]
        above = face(c_ref[0], c_ref[1])
        main = 1.0 + below + above + absorb_of(k, 0)
        rp = 1.0 / main
        f = -above * rp
        dy = rhs_ref[0] * rp
        dv = rp
        w_ref[0] = f
        y_ref[0] = dy
        v_ref[0] = dv
        carry += [above, f, dy, dv]

    def fwd(z, carry):
        out = []
        for n, (rhs_ref, c_ref, y_ref, v_ref, w_ref, k, _) in enumerate(fields):
            below, f_prev, dy_prev, dv_prev = carry[4 * n:4 * n + 4]
            above = face(c_ref[z], c_ref[z + 1])
            main = 1.0 + below + above + absorb_of(k, z)
            pivot = main + below * f_prev
            rp = 1.0 / pivot
            f = -above * rp
            dy = (rhs_ref[z] + below * dy_prev) * rp
            dv = (below * dv_prev) * rp
            w_ref[z] = f
            y_ref[z] = dy
            v_ref[z] = dv
            out += [above, f, dy, dv]
        return tuple(out)

    carry = lax.fori_loop(1, z_cells - 1, fwd, tuple(carry), unroll=8)

    z = z_cells - 1
    back = []
    for n, (rhs_ref, c_ref, y_ref, v_ref, w_ref, k, _) in enumerate(fields):
        below, f_prev, dy_prev, dv_prev = carry[4 * n:4 * n + 4]
        above = hi_ref[k]
        main = 1.0 + below + above + absorb_of(k, z)
        pivot = main + below * f_prev
        rp = 1.0 / pivot
        dy = (rhs_ref[z] + below * dy_prev) * rp
        dv = (below * dv_prev) * rp
        y_ref[z] = dy
        v_ref[z] = dv
        w_ref[z] = rp
        back += [dy, dv, rp]

    def bwd(i, back):
        z = z_cells - 2 - i
        out = []
        for n, (rhs_ref, c_ref, y_ref, v_ref, w_ref, k, _) in enumerate(fields):
            y_next, v_next, w_next = back[3 * n:3 * n + 3]
            f = w_ref[z]
            y_val = y_ref[z] - f * y_next
            v_val = v_ref[z] - f * v_next
            w_val = -f * w_next
            y_ref[z] = y_val
            v_ref[z] = v_val
            w_ref[z] = w_val
            out += [y_val, v_val, w_val]
        return tuple(out)

    back = lax.fori_loop(0, z_cells - 1, bwd, tuple(back), unroll=8)
    for n, (rhs_ref, c_ref, y_ref, v_ref, w_ref, k, _) in enumerate(fields):
        y_first, v_first, w_first = back[3 * n:3 * n + 3]
        beta = beta_ref[k]
        alpha = hi_ref[k]
        pack_ref[0, k] = -v_first * beta
        pack_ref[1, k] = -w_first * alpha
        pack_ref[2, k] = -v_ref[z_cells - 1] * beta
        pack_ref[3, k] = -w_ref[z_cells - 1] * alpha
        pack_ref[4, k] = y_first
        pack_ref[5, k] = y_ref[z_cells - 1]


def local_solve(rhs_temp, rhs_ion, cond_temp, cond_ion, sources, lo, hi, beta):
    shape = jax.ShapeDtypeStruct(rhs_temp.shape, jnp.float32)
    pack = jax.ShapeDtypeStruct((6,) + lo.shape, jnp.float32)
    vmem = pl.BlockSpec(memory_space=pltpu.VMEM)
    return pl.pallas_call(
        local_kernel,
        out_shape=(shape,) * 6 + (pack,),
        in_specs=[vmem] * 8,
        out_specs=(vmem,) * 7,
    )(rhs_temp, rhs_ion, cond_temp, cond_ion, sources, lo, hi, beta)


def chain_solve(packs, rights):
    count = len(packs)
    g1_prev = None
    zl_prev = None
    steps = []
    for i in range(count):
        a, b, c, e = packs[i]
        if g1_prev is None:
            z0 = [yf for yf, yl in rights[i]]
            zl = [yl for yf, yl in rights[i]]
            g0 = b
            g1 = e
        else:
            p = 1.0 - a * g1_prev
            rp = 1.0 / p
            g0 = b * rp
            t = c * g1_prev
            g1 = e + t * g0
            z0 = [(yf - a * zp) * rp for (yf, yl), zp in zip(rights[i], zl_prev)]
            zl = [yl - c * zp + t * z for (yf, yl), zp, z in zip(rights[i], zl_prev, z0)]
        steps.append((g0, g1, z0, zl))
        g1_prev, zl_prev = g1, zl
    firsts = [None] * count
    lasts = [None] * count
    f_next = None
    for i in reversed(range(count)):
        g0, g1, z0, zl = steps[i]
        if f_next is None:
            firsts[i], lasts[i] = z0, zl
        else:
            firsts[i] = [z - g0 * f for z, f in zip(z0, f_next)]
            lasts[i] = [z - g1 * f for z, f in zip(zl, f_next)]
        f_next = firsts[i]
    return firsts, lasts


def gather_ring(pack, size, stride, index):
    chain = lax.axis_size("gz")
    got = {0: pack}
    for s in range(1, size):
        route = []
        for i in range(chain):
            base = i - (i // stride % size) * stride
            route.append((i, base + ((i // stride + s) % size) * stride))
        got[s] = lax.ppermute(pack, "gz", route)
    ordered = []
    for member in range(size):
        pick = got[0]
        for s in range(1, size):
            pick = jnp.where((index - member) % size == s, got[s], pick)
        ordered.append(pick)
    return ordered


def select(values, index):
    out = jnp.zeros_like(values[0])
    for i, value in enumerate(values):
        out = jnp.where(index == i, value, out)
    return out


def deposit(bubble_target, bubble_sink, bubble_void, z_cells, x_cells, y_cells):
    cell_total = z_cells * x_cells
    groups = lax.axis_size("gx")
    target = bubble_target[0]
    record_total = target.shape[0]
    slot_count = 3 * record_total // groups
    width = 2 * y_cells
    payload = jnp.concatenate([bubble_sink[0], bubble_void[0]], axis=1)
    destination = target // cell_total
    cell_index = target % cell_total
    owners = lax.broadcasted_iota(jnp.int32, (record_total, groups), 1)
    owner_hot = (destination[:, None] == owners).astype(jnp.float32)
    row_ids = lax.broadcasted_iota(jnp.int32, (record_total, record_total), 0)
    col_ids = lax.broadcasted_iota(jnp.int32, (record_total, record_total), 1)
    earlier = (row_ids > col_ids).astype(jnp.float32)
    before = jnp.dot(earlier, owner_hot, precision=HIGH)
    rank_within = jnp.sum(before * owner_hot, axis=1).astype(jnp.int32)
    rows_per = slot_count + 1
    out_dest = lax.broadcasted_iota(jnp.int32, (groups, rows_per, 2 * record_total), 0)
    out_slot = lax.broadcasted_iota(jnp.int32, (groups, rows_per, 2 * record_total), 1)
    source = lax.broadcasted_iota(jnp.int32, (groups, rows_per, 2 * record_total), 2)
    record = source % record_total
    dest_of = destination[record]
    rank_of = rank_within[record]
    pick = jnp.where(
        source < record_total,
        (dest_of == out_dest) & (rank_of == out_slot),
        (dest_of == out_dest) & (out_slot == slot_count),
    ).astype(jnp.float32)
    lanes = lax.broadcasted_iota(jnp.int32, (record_total, width), 1)
    cell_plus = (cell_index + 1).astype(jnp.float32)
    cell_lanes = jnp.where(lanes == rank_within[:, None], cell_plus[:, None], 0.0)
    stacked = jnp.concatenate([payload, cell_lanes], axis=0)
    send = jnp.einsum("dsr,rk->dsk", pick, stacked, precision=HIGH)
    received = lax.all_to_all(send, "gx", split_axis=0, concat_axis=0, tiled=True)
    rows = received[:, :slot_count, :].reshape(groups * slot_count, width)
    cells = received[:, slot_count, :slot_count].reshape(groups * slot_count) - 1.0
    cell_ids = lax.broadcasted_iota(jnp.int32, (cell_total, groups * slot_count), 0).astype(jnp.float32)
    spread = (cell_ids == cells[None, :]).astype(jnp.float32)
    sources = jnp.dot(spread, rows, precision=HIGH)
    return sources.reshape(z_cells, x_cells, width)


def body(rhs_temp, rhs_ion, cond_temp, cond_ion, bubble_target, bubble_sink, bubble_void):
    z_cells, x_cells, y_cells = rhs_temp.shape
    chain = lax.axis_size("gz")
    position = lax.axis_index("gz")
    sources = deposit(bubble_target, bubble_sink, bubble_void, z_cells, x_cells, y_cells)

    first = jnp.stack([cond_temp[0], cond_ion[0]])
    last = jnp.stack([cond_temp[-1], cond_ion[-1]])
    from_below = lax.ppermute(last, "gz", [(i, i + 1) for i in range(chain - 1)])
    from_above = lax.ppermute(first, "gz", [(i + 1, i) for i in range(chain - 1)])
    lo = jnp.where(position == 0, 2.0 * first, face(from_below, first))
    hi = jnp.where(position == chain - 1, 0.0, face(last, from_above))

    beta = jnp.where(position == 0, 0.0, lo)
    alpha = hi
    yt, yi, vt, vi, wt, wi, pack = local_solve(
        rhs_temp, rhs_ion, cond_temp, cond_ion, sources, lo, hi, beta
    )
    size = 4 if chain % 4 == 0 and chain > 4 else chain
    groups_z = chain // size
    member = position % size
    group = position // size
    zero = jnp.zeros_like(lo)

    members = gather_ring(pack, size, 1, member)
    packs, rights = [], []
    for r, m in enumerate(members):
        a, b, c, e, yf, yl = (m[j] for j in range(6))
        right_sets = [(yf, yl), (zero, zero), (zero, zero)]
        if r == 0:
            right_sets[1] = (-a, -c)
            a, c = zero, zero
        if r == size - 1:
            right_sets[2] = (-b, -e)
            b, e = zero, zero
        packs.append((a, b, c, e))
        rights.append(right_sets)
    firsts, lasts = chain_solve(packs, rights)
    if groups_z > 1:
        group_pack = jnp.stack([
            -firsts[0][1], -firsts[0][2], -lasts[-1][1], -lasts[-1][2], firsts[0][0], lasts[-1][0]
        ])
        tops = gather_ring(group_pack, groups_z, size, group)
        gpacks = [(t[0], t[1], t[2], t[3]) for t in tops]
        grights = [[(t[4], t[5])] for t in tops]
        gfirsts, glasts = chain_solve(gpacks, grights)
        outside_low = select([zero] + [l[0] for l in glasts[:-1]], group)
        outside_high = select([f[0] for f in gfirsts[1:]] + [zero], group)
    else:
        outside_low = zero
        outside_high = zero

    def value(parts):
        return parts[0] + outside_low * parts[1] + outside_high * parts[2]

    last_prev = select([outside_low] + [value(l) for l in lasts[:-1]], member)
    first_next = select([value(f) for f in firsts[1:]] + [outside_high], member)
    y = (yt, yi)
    v = (vt, vi)
    w = (wt, wi)
    outs = []
    for k in range(2):
        outs.append(
            y[k]
            + v[k] * (beta[k] * last_prev[k])[None]
            + w[k] * (alpha[k] * first_next[k])[None]
        )
    return tuple(outs)


def solution(mesh):
    in_specs = (
        P("gz", "gx", None),
        P("gz", "gx", None),
        P("gz", "gx", None),
        P("gz", "gx", None),
        P("gz", "gx"),
        P("gz", "gx", None),
        P("gz", "gx", None),
    )
    out_specs = (P("gz", "gx", None), P("gz", "gx", None))
    return jax.shard_map(body, mesh=mesh, in_specs=in_specs, out_specs=out_specs, check_vma=False)
```

```python
import functools

import jax
import jax.numpy as jnp
from jax import lax
from jax.experimental import pallas as pl
from jax.experimental.pallas import tpu as pltpu
from jax.sharding import PartitionSpec as P

ion_rate = 40.0
HIGH = lax.Precision.HIGH


def face(lower, upper):
    return 2.0 * lower * upper / (lower + upper)


def local_kernel(rt_ref, ri_ref, ct_ref, ci_ref, src_ref, lo_ref, hi_ref, beta_ref,
                 yt_ref, yi_ref, vt_ref, vi_ref, wt_ref, wi_ref, pack_ref):
    z_cells = rt_ref.shape[0]
    y_cells = rt_ref.shape[2]
    fields = (
        (rt_ref, ct_ref, yt_ref, vt_ref, wt_ref, 0, 1.0),
        (ri_ref, ci_ref, yi_ref, vi_ref, wi_ref, 1, ion_rate),
    )

    def absorb_of(k, z):
        part = src_ref[z, :, k * y_cells:(k + 1) * y_cells]
        return part if k == 0 else ion_rate * part

    carry = []
    for rhs_ref, c_ref, y_ref, v_ref, w_ref, k, _ in fields:
        below = lo_ref[k]
        above = face(c_ref[0], c_ref[1])
        main = 1.0 + below + above + absorb_of(k, 0)
        rp = 1.0 / main
        f = -above * rp
        dy = rhs_ref[0] * rp
        dv = rp
        w_ref[0] = f
        y_ref[0] = dy
        v_ref[0] = dv
        carry += [above, f, dy, dv]

    def fwd(z, carry):
        out = []
        for n, (rhs_ref, c_ref, y_ref, v_ref, w_ref, k, _) in enumerate(fields):
            below, f_prev, dy_prev, dv_prev = carry[4 * n:4 * n + 4]
            above = face(c_ref[z], c_ref[z + 1])
            main = 1.0 + below + above + absorb_of(k, z)
            pivot = main + below * f_prev
            rp = 1.0 / pivot
            f = -above * rp
            dy = (rhs_ref[z] + below * dy_prev) * rp
            dv = (below * dv_prev) * rp
            w_ref[z] = f
            y_ref[z] = dy
            v_ref[z] = dv
            out += [above, f, dy, dv]
        return tuple(out)

    carry = lax.fori_loop(1, z_cells - 1, fwd, tuple(carry), unroll=8)

    z = z_cells - 1
    back = []
    for n, (rhs_ref, c_ref, y_ref, v_ref, w_ref, k, _) in enumerate(fields):
        below, f_prev, dy_prev, dv_prev = carry[4 * n:4 * n + 4]
        above = hi_ref[k]
        main = 1.0 + below + above + absorb_of(k, z)
        pivot = main + below * f_prev
        rp = 1.0 / pivot
        dy = (rhs_ref[z] + below * dy_prev) * rp
        dv = (below * dv_prev) * rp
        y_ref[z] = dy
        v_ref[z] = dv
        w_ref[z] = rp
        back += [dy, dv, rp]

    def bwd(i, back):
        z = z_cells - 2 - i
        out = []
        for n, (rhs_ref, c_ref, y_ref, v_ref, w_ref, k, _) in enumerate(fields):
            y_next, v_next, w_next = back[3 * n:3 * n + 3]
            f = w_ref[z]
            y_val = y_ref[z] - f * y_next
            v_val = v_ref[z] - f * v_next
            w_val = -f * w_next
            y_ref[z] = y_val
            v_ref[z] = v_val
            w_ref[z] = w_val
            out += [y_val, v_val, w_val]
        return tuple(out)

    back = lax.fori_loop(0, z_cells - 1, bwd, tuple(back), unroll=8)
    for n, (rhs_ref, c_ref, y_ref, v_ref, w_ref, k, _) in enumerate(fields):
        y_first, v_first, w_first = back[3 * n:3 * n + 3]
        beta = beta_ref[k]
        alpha = hi_ref[k]
        pack_ref[0, k] = -v_first * beta
        pack_ref[1, k] = -w_first * alpha
        pack_ref[2, k] = -v_ref[z_cells - 1] * beta
        pack_ref[3, k] = -w_ref[z_cells - 1] * alpha
        pack_ref[4, k] = y_first
        pack_ref[5, k] = y_ref[z_cells - 1]


def local_solve(rhs_temp, rhs_ion, cond_temp, cond_ion, sources, lo, hi, beta):
    shape = jax.ShapeDtypeStruct(rhs_temp.shape, jnp.float32)
    pack = jax.ShapeDtypeStruct((6,) + lo.shape, jnp.float32)
    vmem = pl.BlockSpec(memory_space=pltpu.VMEM)
    return pl.pallas_call(
        local_kernel,
        out_shape=(shape,) * 6 + (pack,),
        in_specs=[vmem] * 8,
        out_specs=(vmem,) * 7,
    )(rhs_temp, rhs_ion, cond_temp, cond_ion, sources, lo, hi, beta)


def chain_solve(packs, rights):
    count = len(packs)
    g1_prev = None
    zl_prev = None
    steps = []
    for i in range(count):
        a, b, c, e = packs[i]
        if g1_prev is None:
            z0 = [yf for yf, yl in rights[i]]
            zl = [yl for yf, yl in rights[i]]
            g0 = b
            g1 = e
        else:
            p = 1.0 - a * g1_prev
            rp = 1.0 / p
            g0 = b * rp
            t = c * g1_prev
            g1 = e + t * g0
            z0 = [(yf - a * zp) * rp for (yf, yl), zp in zip(rights[i], zl_prev)]
            zl = [yl - c * zp + t * z for (yf, yl), zp, z in zip(rights[i], zl_prev, z0)]
        steps.append((g0, g1, z0, zl))
        g1_prev, zl_prev = g1, zl
    firsts = [None] * count
    lasts = [None] * count
    f_next = None
    for i in reversed(range(count)):
        g0, g1, z0, zl = steps[i]
        if f_next is None:
            firsts[i], lasts[i] = z0, zl
        else:
            firsts[i] = [z - g0 * f for z, f in zip(z0, f_next)]
            lasts[i] = [z - g1 * f for z, f in zip(zl, f_next)]
        f_next = firsts[i]
    return firsts, lasts


def gather_ring(pack, size, stride, index):
    chain = lax.axis_size("gz")
    got = {0: pack}
    for s in range(1, size):
        route = []
        for i in range(chain):
            base = i - (i // stride % size) * stride
            route.append((i, base + ((i // stride + s) % size) * stride))
        got[s] = lax.ppermute(pack, "gz", route)
    ordered = []
    for member in range(size):
        pick = got[0]
        for s in range(1, size):
            pick = jnp.where((index - member) % size == s, got[s], pick)
        ordered.append(pick)
    return ordered


def select(values, index):
    out = jnp.zeros_like(values[0])
    for i, value in enumerate(values):
        out = jnp.where(index == i, value, out)
    return out


def deposit(bubble_target, bubble_sink, bubble_void, z_cells, x_cells, y_cells):
    cell_total = z_cells * x_cells
    groups = lax.axis_size("gx")
    target = bubble_target[0]
    record_total = target.shape[0]
    slot_count = 3 * record_total // groups
    width = 2 * y_cells
    payload = jnp.concatenate([bubble_sink[0], bubble_void[0]], axis=1)
    destination = target // cell_total
    cell_index = target % cell_total
    owners = lax.broadcasted_iota(jnp.int32, (record_total, groups), 1)
    owner_hot = (destination[:, None] == owners).astype(jnp.float32)
    row_ids = lax.broadcasted_iota(jnp.int32, (record_total, record_total), 0)
    col_ids = lax.broadcasted_iota(jnp.int32, (record_total, record_total), 1)
    earlier = (row_ids > col_ids).astype(jnp.float32)
    before = jnp.dot(earlier, owner_hot, precision=HIGH)
    rank_within = jnp.sum(before * owner_hot, axis=1).astype(jnp.int32)
    rows_per = slot_count + 1
    out_dest = lax.broadcasted_iota(jnp.int32, (groups, rows_per, record_total), 0)
    out_slot = lax.broadcasted_iota(jnp.int32, (groups, rows_per, record_total), 1)
    mine = destination[None, None, :] == out_dest
    pick = jnp.concatenate(
        [mine & (rank_within[None, None, :] == out_slot), mine & (out_slot == slot_count)], axis=2
    ).astype(jnp.float32)
    lanes = lax.broadcasted_iota(jnp.int32, (record_total, width), 1)
    cell_plus = (cell_index + 1).astype(jnp.float32)
    cell_lanes = jnp.where(lanes == rank_within[:, None], cell_plus[:, None], 0.0)
    stacked = jnp.concatenate([payload, cell_lanes], axis=0)
    send = jnp.einsum("dsr,rk->dsk", pick, stacked, precision=HIGH)
    received = lax.all_to_all(send, "gx", split_axis=0, concat_axis=0, tiled=True)
    rows = received[:, :slot_count, :].reshape(groups * slot_count, width)
    cells = received[:, slot_count, :slot_count].reshape(groups * slot_count) - 1.0
    cell_ids = lax.broadcasted_iota(jnp.int32, (cell_total, groups * slot_count), 0).astype(jnp.float32)
    spread = (cell_ids == cells[None, :]).astype(jnp.float32)
    sources = jnp.dot(spread, rows, precision=HIGH)
    return sources.reshape(z_cells, x_cells, width)


def body(rhs_temp, rhs_ion, cond_temp, cond_ion, bubble_target, bubble_sink, bubble_void):
    z_cells, x_cells, y_cells = rhs_temp.shape
    chain = lax.axis_size("gz")
    position = lax.axis_index("gz")
    sources = deposit(bubble_target, bubble_sink, bubble_void, z_cells, x_cells, y_cells)

    first = jnp.stack([cond_temp[0], cond_ion[0]])
    last = jnp.stack([cond_temp[-1], cond_ion[-1]])
    from_below = lax.ppermute(last, "gz", [(i, i + 1) for i in range(chain - 1)])
    from_above = lax.ppermute(first, "gz", [(i + 1, i) for i in range(chain - 1)])
    lo = jnp.where(position == 0, 2.0 * first, face(from_below, first))
    hi = jnp.where(position == chain - 1, 0.0, face(last, from_above))

    beta = jnp.where(position == 0, 0.0, lo)
    alpha = hi
    yt, yi, vt, vi, wt, wi, pack = local_solve(
        rhs_temp, rhs_ion, cond_temp, cond_ion, sources, lo, hi, beta
    )
    size = 4 if chain % 4 == 0 and chain > 4 else chain
    groups_z = chain // size
    member = position % size
    group = position // size
    zero = jnp.zeros_like(lo)

    members = gather_ring(pack, size, 1, member)
    packs, rights = [], []
    for r, m in enumerate(members):
        a, b, c, e, yf, yl = (m[j] for j in range(6))
        right_sets = [(yf, yl), (zero, zero), (zero, zero)]
        if r == 0:
            right_sets[1] = (-a, -c)
            a, c = zero, zero
        if r == size - 1:
            right_sets[2] = (-b, -e)
            b, e = zero, zero
        packs.append((a, b, c, e))
        rights.append(right_sets)
    firsts, lasts = chain_solve(packs, rights)
    if groups_z > 1:
        group_pack = jnp.stack([
            -firsts[0][1], -firsts[0][2], -lasts[-1][1], -lasts[-1][2], firsts[0][0], lasts[-1][0]
        ])
        tops = gather_ring(group_pack, groups_z, size, group)
        gpacks = [(t[0], t[1], t[2], t[3]) for t in tops]
        grights = [[(t[4], t[5])] for t in tops]
        gfirsts, glasts = chain_solve(gpacks, grights)
        outside_low = select([zero] + [l[0] for l in glasts[:-1]], group)
        outside_high = select([f[0] for f in gfirsts[1:]] + [zero], group)
    else:
        outside_low = zero
        outside_high = zero

    def value(parts):
        return parts[0] + outside_low * parts[1] + outside_high * parts[2]

    last_prev = select([outside_low] + [value(l) for l in lasts[:-1]], member)
    first_next = select([value(f) for f in firsts[1:]] + [outside_high], member)
    y = (yt, yi)
    v = (vt, vi)
    w = (wt, wi)
    outs = []
    for k in range(2):
        outs.append(
            y[k]
            + v[k] * (beta[k] * last_prev[k])[None]
            + w[k] * (alpha[k] * first_next[k])[None]
        )
    return tuple(outs)


def solution(mesh):
    in_specs = (
        P("gz", "gx", None),
        P("gz", "gx", None),
        P("gz", "gx", None),
        P("gz", "gx", None),
        P("gz", "gx"),
        P("gz", "gx", None),
        P("gz", "gx", None),
    )
    out_specs = (P("gz", "gx", None), P("gz", "gx", None))
    return jax.shard_map(body, mesh=mesh, in_specs=in_specs, out_specs=out_specs, check_vma=False)
```

```python
import functools

import jax
import jax.numpy as jnp
from jax import lax
from jax.experimental import pallas as pl
from jax.experimental.pallas import tpu as pltpu
from jax.sharding import PartitionSpec as P

ion_rate = 40.0
HIGH = lax.Precision.HIGH


def face(lower, upper):
    return 2.0 * lower * upper / (lower + upper)


CHUNKS = 4


def local_kernel(rt_hbm, ri_hbm, ct_hbm, ci_hbm, src_hbm, lo_ref, hi_ref, beta_ref,
                 yt_hbm, yi_hbm, vt_hbm, vi_hbm, wt_hbm, wi_hbm, pack_ref,
                 rt_ref, ri_ref, ct_ref, ci_ref, src_ref,
                 yt_ref, yi_ref, vt_ref, vi_ref, wt_ref, wi_ref, in_sem, out_sem):
    z_cells = rt_ref.shape[0]
    y_cells = rt_ref.shape[2]
    rows = z_cells // CHUNKS
    ins = ((rt_hbm, rt_ref), (ri_hbm, ri_ref), (src_hbm, src_ref), (ct_hbm, ct_ref), (ci_hbm, ci_ref))
    outs = ((yt_ref, yt_hbm), (yi_ref, yi_hbm), (vt_ref, vt_hbm), (vi_ref, vi_hbm), (wt_ref, wt_hbm), (wi_ref, wi_hbm))

    def copy_in(i, c):
        src_of, dst_of = ins[i]
        return pltpu.make_async_copy(
            src_of.at[pl.ds(c * rows, rows)], dst_of.at[pl.ds(c * rows, rows)], in_sem.at[i, c]
        )

    def copy_out(j, c):
        src_of, dst_of = outs[j]
        return pltpu.make_async_copy(
            src_of.at[pl.ds(c * rows, rows)], dst_of.at[pl.ds(c * rows, rows)], out_sem.at[j, c]
        )

    for c in range(CHUNKS):
        for i in (3, 4, 0, 1, 2):
            copy_in(i, c).start()

    cond_ready = set()

    def wait_chunk(c):
        for cc in (c, c + 1):
            if cc < CHUNKS and cc not in cond_ready:
                copy_in(3, cc).wait()
                copy_in(4, cc).wait()
                cond_ready.add(cc)
        for i in (0, 1, 2):
            copy_in(i, c).wait()

    fields = (
        (rt_ref, ct_ref, yt_ref, vt_ref, wt_ref, 0),
        (ri_ref, ci_ref, yi_ref, vi_ref, wi_ref, 1),
    )

    def absorb_of(k, z):
        part = src_ref[z, :, k * y_cells:(k + 1) * y_cells]
        return part if k == 0 else ion_rate * part

    wait_chunk(0)
    carry = []
    for rhs_ref, c_ref, y_ref, v_ref, w_ref, k in fields:
        below = lo_ref[k]
        above = face(c_ref[0], c_ref[1])
        main = 1.0 + below + above + absorb_of(k, 0)
        rp = 1.0 / main
        f = -above * rp
        dy = rhs_ref[0] * rp
        dv = rp
        w_ref[0] = f
        y_ref[0] = dy
        v_ref[0] = dv
        carry += [above, f, dy, dv]

    def fwd(z, carry):
        out = []
        for n, (rhs_ref, c_ref, y_ref, v_ref, w_ref, k) in enumerate(fields):
            below, f_prev, dy_prev, dv_prev = carry[4 * n:4 * n + 4]
            above = face(c_ref[z], c_ref[z + 1])
            main = 1.0 + below + above + absorb_of(k, z)
            pivot = main + below * f_prev
            rp = 1.0 / pivot
            f = -above * rp
            dy = (rhs_ref[z] + below * dy_prev) * rp
            dv = (below * dv_prev) * rp
            w_ref[z] = f
            y_ref[z] = dy
            v_ref[z] = dv
            out += [above, f, dy, dv]
        return tuple(out)

    carry = tuple(carry)
    for c in range(CHUNKS):
        if c > 0:
            wait_chunk(c)
        low = max(1, c * rows)
        high = min(z_cells - 1, (c + 1) * rows)
        carry = lax.fori_loop(low, high, fwd, carry, unroll=8)

    z = z_cells - 1
    back = []
    for n, (rhs_ref, c_ref, y_ref, v_ref, w_ref, k) in enumerate(fields):
        below, f_prev, dy_prev, dv_prev = carry[4 * n:4 * n + 4]
        above = hi_ref[k]
        main = 1.0 + below + above + absorb_of(k, z)
        pivot = main + below * f_prev
        rp = 1.0 / pivot
        dy = (rhs_ref[z] + below * dy_prev) * rp
        dv = (below * dv_prev) * rp
        y_ref[z] = dy
        v_ref[z] = dv
        w_ref[z] = rp
        back += [dy, dv, rp]

    def bwd(z, back):
        out = []
        for n, (rhs_ref, c_ref, y_ref, v_ref, w_ref, k) in enumerate(fields):
            y_next, v_next, w_next = back[3 * n:3 * n + 3]
            f = w_ref[z]
            y_val = y_ref[z] - f * y_next
            v_val = v_ref[z] - f * v_next
            w_val = -f * w_next
            y_ref[z] = y_val
            v_ref[z] = v_val
            w_ref[z] = w_val
            out += [y_val, v_val, w_val]
        return tuple(out)

    back = tuple(back)
    for c in reversed(range(CHUNKS)):
        low = c * rows
        high = min(z_cells - 1, (c + 1) * rows)
        back = lax.fori_loop(
            0, high - low, lambda i, b: bwd(high - 1 - i, b), back, unroll=8
        )
        for j in range(6):
            copy_out(j, c).start()
    for n, (rhs_ref, c_ref, y_ref, v_ref, w_ref, k) in enumerate(fields):
        y_first, v_first, w_first = back[3 * n:3 * n + 3]
        beta = beta_ref[k]
        alpha = hi_ref[k]
        pack_ref[0, k] = -v_first * beta
        pack_ref[1, k] = -w_first * alpha
        pack_ref[2, k] = -v_ref[z_cells - 1] * beta
        pack_ref[3, k] = -w_ref[z_cells - 1] * alpha
        pack_ref[4, k] = y_first
        pack_ref[5, k] = y_ref[z_cells - 1]
    for c in range(CHUNKS):
        for j in range(6):
            copy_out(j, c).wait()


def local_solve(rhs_temp, rhs_ion, cond_temp, cond_ion, sources, lo, hi, beta):
    shape = jax.ShapeDtypeStruct(rhs_temp.shape, jnp.float32)
    pack = jax.ShapeDtypeStruct((6,) + lo.shape, jnp.float32)
    vmem = pl.BlockSpec(memory_space=pltpu.VMEM)
    hbm = pl.BlockSpec(memory_space=pl.ANY)
    plane = pltpu.VMEM(rhs_temp.shape, jnp.float32)
    return pl.pallas_call(
        local_kernel,
        out_shape=(shape,) * 6 + (pack,),
        in_specs=[hbm] * 5 + [vmem] * 3,
        out_specs=(hbm,) * 6 + (vmem,),
        scratch_shapes=[plane] * 4
        + [pltpu.VMEM(sources.shape, jnp.float32)]
        + [plane] * 6
        + [pltpu.SemaphoreType.DMA((5, CHUNKS)), pltpu.SemaphoreType.DMA((6, CHUNKS))],
    )(rhs_temp, rhs_ion, cond_temp, cond_ion, sources, lo, hi, beta)


def chain_solve(packs, rights):
    count = len(packs)
    g1_prev = None
    zl_prev = None
    steps = []
    for i in range(count):
        a, b, c, e = packs[i]
        if g1_prev is None:
            z0 = [yf for yf, yl in rights[i]]
            zl = [yl for yf, yl in rights[i]]
            g0 = b
            g1 = e
        else:
            p = 1.0 - a * g1_prev
            rp = 1.0 / p
            g0 = b * rp
            t = c * g1_prev
            g1 = e + t * g0
            z0 = [(yf - a * zp) * rp for (yf, yl), zp in zip(rights[i], zl_prev)]
            zl = [yl - c * zp + t * z for (yf, yl), zp, z in zip(rights[i], zl_prev, z0)]
        steps.append((g0, g1, z0, zl))
        g1_prev, zl_prev = g1, zl
    firsts = [None] * count
    lasts = [None] * count
    f_next = None
    for i in reversed(range(count)):
        g0, g1, z0, zl = steps[i]
        if f_next is None:
            firsts[i], lasts[i] = z0, zl
        else:
            firsts[i] = [z - g0 * f for z, f in zip(z0, f_next)]
            lasts[i] = [z - g1 * f for z, f in zip(zl, f_next)]
        f_next = firsts[i]
    return firsts, lasts


def gather_ring(pack, size, stride, index):
    chain = lax.axis_size("gz")
    got = {0: pack}
    for s in range(1, size):
        route = []
        for i in range(chain):
            base = i - (i // stride % size) * stride
            route.append((i, base + ((i // stride + s) % size) * stride))
        got[s] = lax.ppermute(pack, "gz", route)
    ordered = []
    for member in range(size):
        pick = got[0]
        for s in range(1, size):
            pick = jnp.where((index - member) % size == s, got[s], pick)
        ordered.append(pick)
    return ordered


def select(values, index):
    out = jnp.zeros_like(values[0])
    for i, value in enumerate(values):
        out = jnp.where(index == i, value, out)
    return out


def deposit(bubble_target, bubble_sink, bubble_void, z_cells, x_cells, y_cells):
    cell_total = z_cells * x_cells
    groups = lax.axis_size("gx")
    target = bubble_target[0]
    record_total = target.shape[0]
    slot_count = 3 * record_total // groups
    width = 2 * y_cells
    payload = jnp.concatenate([bubble_sink[0], bubble_void[0]], axis=1)
    destination = target // cell_total
    cell_index = target % cell_total
    owners = lax.broadcasted_iota(jnp.int32, (record_total, groups), 1)
    owner_hot = (destination[:, None] == owners).astype(jnp.float32)
    row_ids = lax.broadcasted_iota(jnp.int32, (record_total, record_total), 0)
    col_ids = lax.broadcasted_iota(jnp.int32, (record_total, record_total), 1)
    earlier = (row_ids > col_ids).astype(jnp.float32)
    before = jnp.dot(earlier, owner_hot, precision=HIGH)
    rank_within = jnp.sum(before * owner_hot, axis=1).astype(jnp.int32)
    rows_per = slot_count + 1
    out_dest = lax.broadcasted_iota(jnp.int32, (groups, rows_per, record_total), 0)
    out_slot = lax.broadcasted_iota(jnp.int32, (groups, rows_per, record_total), 1)
    mine = destination[None, None, :] == out_dest
    pick = jnp.concatenate(
        [mine & (rank_within[None, None, :] == out_slot), mine & (out_slot == slot_count)], axis=2
    ).astype(jnp.float32)
    lanes = lax.broadcasted_iota(jnp.int32, (record_total, width), 1)
    cell_plus = (cell_index + 1).astype(jnp.float32)
    cell_lanes = jnp.where(lanes == rank_within[:, None], cell_plus[:, None], 0.0)
    stacked = jnp.concatenate([payload, cell_lanes], axis=0)
    send = jnp.einsum("dsr,rk->dsk", pick, stacked, precision=HIGH)
    received = lax.all_to_all(send, "gx", split_axis=0, concat_axis=0, tiled=True)
    rows = received[:, :slot_count, :].reshape(groups * slot_count, width)
    cells = received[:, slot_count, :slot_count].reshape(groups * slot_count) - 1.0
    cell_ids = lax.broadcasted_iota(jnp.int32, (cell_total, groups * slot_count), 0).astype(jnp.float32)
    spread = (cell_ids == cells[None, :]).astype(jnp.float32)
    sources = jnp.dot(spread, rows, precision=HIGH)
    return sources.reshape(z_cells, x_cells, width)


def body(rhs_temp, rhs_ion, cond_temp, cond_ion, bubble_target, bubble_sink, bubble_void):
    z_cells, x_cells, y_cells = rhs_temp.shape
    chain = lax.axis_size("gz")
    position = lax.axis_index("gz")
    sources = deposit(bubble_target, bubble_sink, bubble_void, z_cells, x_cells, y_cells)

    first = jnp.stack([cond_temp[0], cond_ion[0]])
    last = jnp.stack([cond_temp[-1], cond_ion[-1]])
    from_below = lax.ppermute(last, "gz", [(i, i + 1) for i in range(chain - 1)])
    from_above = lax.ppermute(first, "gz", [(i + 1, i) for i in range(chain - 1)])
    lo = jnp.where(position == 0, 2.0 * first, face(from_below, first))
    hi = jnp.where(position == chain - 1, 0.0, face(last, from_above))

    beta = jnp.where(position == 0, 0.0, lo)
    alpha = hi
    yt, yi, vt, vi, wt, wi, pack = local_solve(
        rhs_temp, rhs_ion, cond_temp, cond_ion, sources, lo, hi, beta
    )
    size = 4 if chain % 4 == 0 and chain > 4 else chain
    groups_z = chain // size
    member = position % size
    group = position // size
    zero = jnp.zeros_like(lo)

    members = gather_ring(pack, size, 1, member)
    packs, rights = [], []
    for r, m in enumerate(members):
        a, b, c, e, yf, yl = (m[j] for j in range(6))
        right_sets = [(yf, yl), (zero, zero), (zero, zero)]
        if r == 0:
            right_sets[1] = (-a, -c)
            a, c = zero, zero
        if r == size - 1:
            right_sets[2] = (-b, -e)
            b, e = zero, zero
        packs.append((a, b, c, e))
        rights.append(right_sets)
    firsts, lasts = chain_solve(packs, rights)
    if groups_z > 1:
        group_pack = jnp.stack([
            -firsts[0][1], -firsts[0][2], -lasts[-1][1], -lasts[-1][2], firsts[0][0], lasts[-1][0]
        ])
        tops = gather_ring(group_pack, groups_z, size, group)
        gpacks = [(t[0], t[1], t[2], t[3]) for t in tops]
        grights = [[(t[4], t[5])] for t in tops]
        gfirsts, glasts = chain_solve(gpacks, grights)
        outside_low = select([zero] + [l[0] for l in glasts[:-1]], group)
        outside_high = select([f[0] for f in gfirsts[1:]] + [zero], group)
    else:
        outside_low = zero
        outside_high = zero

    def value(parts):
        return parts[0] + outside_low * parts[1] + outside_high * parts[2]

    last_prev = select([outside_low] + [value(l) for l in lasts[:-1]], member)
    first_next = select([value(f) for f in firsts[1:]] + [outside_high], member)
    y = (yt, yi)
    v = (vt, vi)
    w = (wt, wi)
    outs = []
    for k in range(2):
        outs.append(
            y[k]
            + v[k] * (beta[k] * last_prev[k])[None]
            + w[k] * (alpha[k] * first_next[k])[None]
        )
    return tuple(outs)


def solution(mesh):
    in_specs = (
        P("gz", "gx", None),
        P("gz", "gx", None),
        P("gz", "gx", None),
        P("gz", "gx", None),
        P("gz", "gx"),
        P("gz", "gx", None),
        P("gz", "gx", None),
    )
    out_specs = (P("gz", "gx", None), P("gz", "gx", None))
    return jax.shard_map(body, mesh=mesh, in_specs=in_specs, out_specs=out_specs, check_vma=False)
```

```python
import functools

import jax
import jax.numpy as jnp
from jax import lax
from jax.experimental import pallas as pl
from jax.experimental.pallas import tpu as pltpu
from jax.sharding import PartitionSpec as P

ion_rate = 40.0
HIGH = lax.Precision.HIGH


def face(lower, upper):
    return 2.0 * lower * upper / (lower + upper)


def local_kernel(rt_ref, ri_ref, ct_ref, ci_ref, mt_ref, mi_ref, src_ref, lo_ref, hi_ref, beta_ref,
                 yt_ref, yi_ref, vt_ref, vi_ref, wt_ref, wi_ref, pack_ref):
    z_cells = rt_ref.shape[0]
    y_cells = rt_ref.shape[2]
    fields = (
        (rt_ref, ct_ref, yt_ref, vt_ref, wt_ref, 0, mt_ref),
        (ri_ref, ci_ref, yi_ref, vi_ref, wi_ref, 1, mi_ref),
    )

    def absorb_of(k, z):
        part = src_ref[z, :, k * y_cells:(k + 1) * y_cells]
        return part if k == 0 else ion_rate * part

    carry = []
    for rhs_ref, c_ref, y_ref, v_ref, w_ref, k, _ in fields:
        below = lo_ref[k]
        above = c_ref[0]
        main = 1.0 + below + above + absorb_of(k, 0)
        rp = 1.0 / main
        f = -above * rp
        dy = rhs_ref[0] * rp
        dv = rp
        w_ref[0] = f
        y_ref[0] = dy
        v_ref[0] = dv
        carry += [above, f, dy, dv]

    def fwd(z, carry):
        out = []
        for n, (rhs_ref, c_ref, y_ref, v_ref, w_ref, k, m_ref) in enumerate(fields):
            below, f_prev, dy_prev, dv_prev = carry[4 * n:4 * n + 4]
            above = c_ref[z]
            main = m_ref[z] + absorb_of(k, z)
            pivot = main + below * f_prev
            rp = 1.0 / pivot
            f = -above * rp
            dy = (rhs_ref[z] + below * dy_prev) * rp
            dv = (below * dv_prev) * rp
            w_ref[z] = f
            y_ref[z] = dy
            v_ref[z] = dv
            out += [above, f, dy, dv]
        return tuple(out)

    carry = lax.fori_loop(1, z_cells - 1, fwd, tuple(carry), unroll=8)

    z = z_cells - 1
    back = []
    for n, (rhs_ref, c_ref, y_ref, v_ref, w_ref, k, _) in enumerate(fields):
        below, f_prev, dy_prev, dv_prev = carry[4 * n:4 * n + 4]
        above = hi_ref[k]
        main = 1.0 + below + above + absorb_of(k, z)
        pivot = main + below * f_prev
        rp = 1.0 / pivot
        dy = (rhs_ref[z] + below * dy_prev) * rp
        dv = (below * dv_prev) * rp
        y_ref[z] = dy
        v_ref[z] = dv
        w_ref[z] = rp
        back += [dy, dv, rp]

    def bwd(i, back):
        z = z_cells - 2 - i
        out = []
        for n, (rhs_ref, c_ref, y_ref, v_ref, w_ref, k, _) in enumerate(fields):
            y_next, v_next, w_next = back[3 * n:3 * n + 3]
            f = w_ref[z]
            y_val = y_ref[z] - f * y_next
            v_val = v_ref[z] - f * v_next
            w_val = -f * w_next
            y_ref[z] = y_val
            v_ref[z] = v_val
            w_ref[z] = w_val
            out += [y_val, v_val, w_val]
        return tuple(out)

    back = lax.fori_loop(0, z_cells - 1, bwd, tuple(back), unroll=8)
    for n, (rhs_ref, c_ref, y_ref, v_ref, w_ref, k, _) in enumerate(fields):
        y_first, v_first, w_first = back[3 * n:3 * n + 3]
        beta = beta_ref[k]
        alpha = hi_ref[k]
        pack_ref[0, k] = -v_first * beta
        pack_ref[1, k] = -w_first * alpha
        pack_ref[2, k] = -v_ref[z_cells - 1] * beta
        pack_ref[3, k] = -w_ref[z_cells - 1] * alpha
        pack_ref[4, k] = y_first
        pack_ref[5, k] = y_ref[z_cells - 1]


def local_solve(rhs_temp, rhs_ion, cond_temp, cond_ion, main_temp, main_ion, sources, lo, hi, beta):
    shape = jax.ShapeDtypeStruct(rhs_temp.shape, jnp.float32)
    pack = jax.ShapeDtypeStruct((6,) + lo.shape, jnp.float32)
    vmem = pl.BlockSpec(memory_space=pltpu.VMEM)
    return pl.pallas_call(
        local_kernel,
        out_shape=(shape,) * 6 + (pack,),
        in_specs=[vmem] * 10,
        out_specs=(vmem,) * 7,
    )(rhs_temp, rhs_ion, cond_temp, cond_ion, main_temp, main_ion, sources, lo, hi, beta)


def chain_solve(packs, rights):
    count = len(packs)
    g1_prev = None
    zl_prev = None
    steps = []
    for i in range(count):
        a, b, c, e = packs[i]
        if g1_prev is None:
            z0 = [yf for yf, yl in rights[i]]
            zl = [yl for yf, yl in rights[i]]
            g0 = b
            g1 = e
        else:
            p = 1.0 - a * g1_prev
            rp = 1.0 / p
            g0 = b * rp
            t = c * g1_prev
            g1 = e + t * g0
            z0 = [(yf - a * zp) * rp for (yf, yl), zp in zip(rights[i], zl_prev)]
            zl = [yl - c * zp + t * z for (yf, yl), zp, z in zip(rights[i], zl_prev, z0)]
        steps.append((g0, g1, z0, zl))
        g1_prev, zl_prev = g1, zl
    firsts = [None] * count
    lasts = [None] * count
    f_next = None
    for i in reversed(range(count)):
        g0, g1, z0, zl = steps[i]
        if f_next is None:
            firsts[i], lasts[i] = z0, zl
        else:
            firsts[i] = [z - g0 * f for z, f in zip(z0, f_next)]
            lasts[i] = [z - g1 * f for z, f in zip(zl, f_next)]
        f_next = firsts[i]
    return firsts, lasts


def gather_ring(pack, size, stride, index):
    chain = lax.axis_size("gz")
    got = {0: pack}
    for s in range(1, size):
        route = []
        for i in range(chain):
            base = i - (i // stride % size) * stride
            route.append((i, base + ((i // stride + s) % size) * stride))
        got[s] = lax.ppermute(pack, "gz", route)
    ordered = []
    for member in range(size):
        pick = got[0]
        for s in range(1, size):
            pick = jnp.where((index - member) % size == s, got[s], pick)
        ordered.append(pick)
    return ordered


def select(values, index):
    out = jnp.zeros_like(values[0])
    for i, value in enumerate(values):
        out = jnp.where(index == i, value, out)
    return out


def deposit(bubble_target, bubble_sink, bubble_void, z_cells, x_cells, y_cells):
    cell_total = z_cells * x_cells
    groups = lax.axis_size("gx")
    target = bubble_target[0]
    record_total = target.shape[0]
    slot_count = 3 * record_total // groups
    width = 2 * y_cells
    payload = jnp.concatenate([bubble_sink[0], bubble_void[0]], axis=1)
    destination = target // cell_total
    cell_index = target % cell_total
    owners = lax.broadcasted_iota(jnp.int32, (record_total, groups), 1)
    owner_hot = (destination[:, None] == owners).astype(jnp.float32)
    row_ids = lax.broadcasted_iota(jnp.int32, (record_total, record_total), 0)
    col_ids = lax.broadcasted_iota(jnp.int32, (record_total, record_total), 1)
    earlier = (row_ids > col_ids).astype(jnp.float32)
    before = jnp.dot(earlier, owner_hot, precision=HIGH)
    rank_within = jnp.sum(before * owner_hot, axis=1).astype(jnp.int32)
    rows_per = slot_count + 1
    out_dest = lax.broadcasted_iota(jnp.int32, (groups, rows_per, record_total), 0)
    out_slot = lax.broadcasted_iota(jnp.int32, (groups, rows_per, record_total), 1)
    mine = destination[None, None, :] == out_dest
    pick = jnp.concatenate(
        [mine & (rank_within[None, None, :] == out_slot), mine & (out_slot == slot_count)], axis=2
    ).astype(jnp.float32)
    lanes = lax.broadcasted_iota(jnp.int32, (record_total, width), 1)
    cell_plus = (cell_index + 1).astype(jnp.float32)
    cell_lanes = jnp.where(lanes == rank_within[:, None], cell_plus[:, None], 0.0)
    stacked = jnp.concatenate([payload, cell_lanes], axis=0)
    send = jnp.einsum("dsr,rk->dsk", pick, stacked, precision=HIGH)
    received = lax.all_to_all(send, "gx", split_axis=0, concat_axis=0, tiled=True)
    rows = received[:, :slot_count, :].reshape(groups * slot_count, width)
    cells = received[:, slot_count, :slot_count].reshape(groups * slot_count) - 1.0
    cell_ids = lax.broadcasted_iota(jnp.int32, (cell_total, groups * slot_count), 0).astype(jnp.float32)
    spread = (cell_ids == cells[None, :]).astype(jnp.float32)
    sources = jnp.dot(spread, rows, precision=HIGH)
    return sources.reshape(z_cells, x_cells, width)


def body(rhs_temp, rhs_ion, cond_temp, cond_ion, bubble_target, bubble_sink, bubble_void):
    z_cells, x_cells, y_cells = rhs_temp.shape
    chain = lax.axis_size("gz")
    position = lax.axis_index("gz")
    sources = deposit(bubble_target, bubble_sink, bubble_void, z_cells, x_cells, y_cells)

    first = jnp.stack([cond_temp[0], cond_ion[0]])
    last = jnp.stack([cond_temp[-1], cond_ion[-1]])
    from_below = lax.ppermute(last, "gz", [(i, i + 1) for i in range(chain - 1)])
    from_above = lax.ppermute(first, "gz", [(i + 1, i) for i in range(chain - 1)])
    lo = jnp.where(position == 0, 2.0 * first, face(from_below, first))
    hi = jnp.where(position == chain - 1, 0.0, face(last, from_above))

    beta = jnp.where(position == 0, 0.0, lo)
    alpha = hi
    faces, mains = [], []
    for cond in (cond_temp, cond_ion):
        inner = face(cond[:-1], cond[1:])
        edge = jnp.zeros_like(cond[:1])
        above = jnp.concatenate([inner, edge])
        faces.append(above)
        mains.append(1.0 + jnp.concatenate([edge, inner]) + above)
    yt, yi, vt, vi, wt, wi, pack = local_solve(
        rhs_temp, rhs_ion, faces[0], faces[1], mains[0], mains[1], sources, lo, hi, beta
    )
    size = 4 if chain % 4 == 0 and chain > 4 else chain
    groups_z = chain // size
    member = position % size
    group = position // size
    zero = jnp.zeros_like(lo)

    members = gather_ring(pack, size, 1, member)
    packs, rights = [], []
    for r, m in enumerate(members):
        a, b, c, e, yf, yl = (m[j] for j in range(6))
        right_sets = [(yf, yl), (zero, zero), (zero, zero)]
        if r == 0:
            right_sets[1] = (-a, -c)
            a, c = zero, zero
        if r == size - 1:
            right_sets[2] = (-b, -e)
            b, e = zero, zero
        packs.append((a, b, c, e))
        rights.append(right_sets)
    firsts, lasts = chain_solve(packs, rights)
    if groups_z > 1:
        group_pack = jnp.stack([
            -firsts[0][1], -firsts[0][2], -lasts[-1][1], -lasts[-1][2], firsts[0][0], lasts[-1][0]
        ])
        tops = gather_ring(group_pack, groups_z, size, group)
        gpacks = [(t[0], t[1], t[2], t[3]) for t in tops]
        grights = [[(t[4], t[5])] for t in tops]
        gfirsts, glasts = chain_solve(gpacks, grights)
        outside_low = select([zero] + [l[0] for l in glasts[:-1]], group)
        outside_high = select([f[0] for f in gfirsts[1:]] + [zero], group)
    else:
        outside_low = zero
        outside_high = zero

    def value(parts):
        return parts[0] + outside_low * parts[1] + outside_high * parts[2]

    last_prev = select([outside_low] + [value(l) for l in lasts[:-1]], member)
    first_next = select([value(f) for f in firsts[1:]] + [outside_high], member)
    y = (yt, yi)
    v = (vt, vi)
    w = (wt, wi)
    outs = []
    for k in range(2):
        outs.append(
            y[k]
            + v[k] * (beta[k] * last_prev[k])[None]
            + w[k] * (alpha[k] * first_next[k])[None]
        )
    return tuple(outs)


def solution(mesh):
    in_specs = (
        P("gz", "gx", None),
        P("gz", "gx", None),
        P("gz", "gx", None),
        P("gz", "gx", None),
        P("gz", "gx"),
        P("gz", "gx", None),
        P("gz", "gx", None),
    )
    out_specs = (P("gz", "gx", None), P("gz", "gx", None))
    return jax.shard_map(body, mesh=mesh, in_specs=in_specs, out_specs=out_specs, check_vma=False)
```

```python
import functools

import jax
import jax.numpy as jnp
from jax import lax
from jax.experimental import pallas as pl
from jax.experimental.pallas import tpu as pltpu
from jax.sharding import PartitionSpec as P

ion_rate = 40.0
HIGH = lax.Precision.HIGH


def face(lower, upper):
    return 2.0 * lower * upper / (lower + upper)


def local_kernel(rt_ref, ri_ref, ct_ref, ci_ref, src_ref, lo_ref, hi_ref, beta_ref,
                 yt_ref, yi_ref, vt_ref, vi_ref, wt_ref, wi_ref, pack_ref):
    z_cells = rt_ref.shape[0]
    y_cells = rt_ref.shape[2]
    fields = (
        (rt_ref, ct_ref, yt_ref, vt_ref, wt_ref, 0, 1.0),
        (ri_ref, ci_ref, yi_ref, vi_ref, wi_ref, 1, ion_rate),
    )

    def absorb_of(k, z):
        part = src_ref[z, :, k * y_cells:(k + 1) * y_cells]
        return part if k == 0 else ion_rate * part

    carry = []
    for rhs_ref, c_ref, y_ref, v_ref, w_ref, k, _ in fields:
        below = lo_ref[k]
        above = face(c_ref[0], c_ref[1])
        main = 1.0 + below + above + absorb_of(k, 0)
        rp = 1.0 / main
        f = -above * rp
        dy = rhs_ref[0] * rp
        dv = rp
        w_ref[0] = f
        y_ref[0] = dy
        v_ref[0] = dv
        carry += [above, f, dy, dv]

    def fwd(z, carry):
        out = []
        for n, (rhs_ref, c_ref, y_ref, v_ref, w_ref, k, _) in enumerate(fields):
            below, f_prev, dy_prev, dv_prev = carry[4 * n:4 * n + 4]
            above = face(c_ref[z], c_ref[z + 1])
            main = 1.0 + below + above + absorb_of(k, z)
            pivot = main + below * f_prev
            rp = 1.0 / pivot
            f = -above * rp
            dy = (rhs_ref[z] + below * dy_prev) * rp
            dv = (below * dv_prev) * rp
            w_ref[z] = f
            y_ref[z] = dy
            v_ref[z] = dv
            out += [above, f, dy, dv]
        return tuple(out)

    carry = lax.fori_loop(1, z_cells - 1, fwd, tuple(carry), unroll=True)

    z = z_cells - 1
    back = []
    for n, (rhs_ref, c_ref, y_ref, v_ref, w_ref, k, _) in enumerate(fields):
        below, f_prev, dy_prev, dv_prev = carry[4 * n:4 * n + 4]
        above = hi_ref[k]
        main = 1.0 + below + above + absorb_of(k, z)
        pivot = main + below * f_prev
        rp = 1.0 / pivot
        dy = (rhs_ref[z] + below * dy_prev) * rp
        dv = (below * dv_prev) * rp
        y_ref[z] = dy
        v_ref[z] = dv
        w_ref[z] = rp
        back += [dy, dv, rp]

    def bwd(i, back):
        z = z_cells - 2 - i
        out = []
        for n, (rhs_ref, c_ref, y_ref, v_ref, w_ref, k, _) in enumerate(fields):
            y_next, v_next, w_next = back[3 * n:3 * n + 3]
            f = w_ref[z]
            y_val = y_ref[z] - f * y_next
            v_val = v_ref[z] - f * v_next
            w_val = -f * w_next
            y_ref[z] = y_val
            v_ref[z] = v_val
            w_ref[z] = w_val
            out += [y_val, v_val, w_val]
        return tuple(out)

    back = lax.fori_loop(0, z_cells - 1, bwd, tuple(back), unroll=True)
    for n, (rhs_ref, c_ref, y_ref, v_ref, w_ref, k, _) in enumerate(fields):
        y_first, v_first, w_first = back[3 * n:3 * n + 3]
        beta = beta_ref[k]
        alpha = hi_ref[k]
        pack_ref[0, k] = -v_first * beta
        pack_ref[1, k] = -w_first * alpha
        pack_ref[2, k] = -v_ref[z_cells - 1] * beta
        pack_ref[3, k] = -w_ref[z_cells - 1] * alpha
        pack_ref[4, k] = y_first
        pack_ref[5, k] = y_ref[z_cells - 1]


def local_solve(rhs_temp, rhs_ion, cond_temp, cond_ion, sources, lo, hi, beta):
    shape = jax.ShapeDtypeStruct(rhs_temp.shape, jnp.float32)
    pack = jax.ShapeDtypeStruct((6,) + lo.shape, jnp.float32)
    vmem = pl.BlockSpec(memory_space=pltpu.VMEM)
    return pl.pallas_call(
        local_kernel,
        out_shape=(shape,) * 6 + (pack,),
        in_specs=[vmem] * 8,
        out_specs=(vmem,) * 7,
    )(rhs_temp, rhs_ion, cond_temp, cond_ion, sources, lo, hi, beta)


def chain_solve(packs, rights):
    count = len(packs)
    g1_prev = None
    zl_prev = None
    steps = []
    for i in range(count):
        a, b, c, e = packs[i]
        if g1_prev is None:
            z0 = [yf for yf, yl in rights[i]]
            zl = [yl for yf, yl in rights[i]]
            g0 = b
            g1 = e
        else:
            p = 1.0 - a * g1_prev
            rp = 1.0 / p
            g0 = b * rp
            t = c * g1_prev
            g1 = e + t * g0
            z0 = [(yf - a * zp) * rp for (yf, yl), zp in zip(rights[i], zl_prev)]
            zl = [yl - c * zp + t * z for (yf, yl), zp, z in zip(rights[i], zl_prev, z0)]
        steps.append((g0, g1, z0, zl))
        g1_prev, zl_prev = g1, zl
    firsts = [None] * count
    lasts = [None] * count
    f_next = None
    for i in reversed(range(count)):
        g0, g1, z0, zl = steps[i]
        if f_next is None:
            firsts[i], lasts[i] = z0, zl
        else:
            firsts[i] = [z - g0 * f for z, f in zip(z0, f_next)]
            lasts[i] = [z - g1 * f for z, f in zip(zl, f_next)]
        f_next = firsts[i]
    return firsts, lasts


def gather_ring(pack, size, stride, index):
    chain = lax.axis_size("gz")
    got = {0: pack}
    for s in range(1, size):
        route = []
        for i in range(chain):
            base = i - (i // stride % size) * stride
            route.append((i, base + ((i // stride + s) % size) * stride))
        got[s] = lax.ppermute(pack, "gz", route)
    ordered = []
    for member in range(size):
        pick = got[0]
        for s in range(1, size):
            pick = jnp.where((index - member) % size == s, got[s], pick)
        ordered.append(pick)
    return ordered


def select(values, index):
    out = jnp.zeros_like(values[0])
    for i, value in enumerate(values):
        out = jnp.where(index == i, value, out)
    return out


def deposit(bubble_target, bubble_sink, bubble_void, z_cells, x_cells, y_cells):
    cell_total = z_cells * x_cells
    groups = lax.axis_size("gx")
    target = bubble_target[0]
    record_total = target.shape[0]
    slot_count = 3 * record_total // groups
    width = 2 * y_cells
    payload = jnp.concatenate([bubble_sink[0], bubble_void[0]], axis=1)
    destination = target // cell_total
    cell_index = target % cell_total
    owners = lax.broadcasted_iota(jnp.int32, (record_total, groups), 1)
    owner_hot = (destination[:, None] == owners).astype(jnp.float32)
    row_ids = lax.broadcasted_iota(jnp.int32, (record_total, record_total), 0)
    col_ids = lax.broadcasted_iota(jnp.int32, (record_total, record_total), 1)
    earlier = (row_ids > col_ids).astype(jnp.float32)
    before = jnp.dot(earlier, owner_hot, precision=HIGH)
    rank_within = jnp.sum(before * owner_hot, axis=1).astype(jnp.int32)
    rows_per = slot_count + 1
    out_dest = lax.broadcasted_iota(jnp.int32, (groups, rows_per, record_total), 0)
    out_slot = lax.broadcasted_iota(jnp.int32, (groups, rows_per, record_total), 1)
    mine = destination[None, None, :] == out_dest
    pick = jnp.concatenate(
        [mine & (rank_within[None, None, :] == out_slot), mine & (out_slot == slot_count)], axis=2
    ).astype(jnp.float32)
    lanes = lax.broadcasted_iota(jnp.int32, (record_total, width), 1)
    cell_plus = (cell_index + 1).astype(jnp.float32)
    cell_lanes = jnp.where(lanes == rank_within[:, None], cell_plus[:, None], 0.0)
    stacked = jnp.concatenate([payload, cell_lanes], axis=0)
    send = jnp.einsum("dsr,rk->dsk", pick, stacked, precision=HIGH)
    received = lax.all_to_all(send, "gx", split_axis=0, concat_axis=0, tiled=True)
    rows = received[:, :slot_count, :].reshape(groups * slot_count, width)
    cells = received[:, slot_count, :slot_count].reshape(groups * slot_count) - 1.0
    cell_ids = lax.broadcasted_iota(jnp.int32, (cell_total, groups * slot_count), 0).astype(jnp.float32)
    spread = (cell_ids == cells[None, :]).astype(jnp.float32)
    sources = jnp.dot(spread, rows, precision=HIGH)
    return sources.reshape(z_cells, x_cells, width)


def body(rhs_temp, rhs_ion, cond_temp, cond_ion, bubble_target, bubble_sink, bubble_void):
    z_cells, x_cells, y_cells = rhs_temp.shape
    chain = lax.axis_size("gz")
    position = lax.axis_index("gz")
    sources = deposit(bubble_target, bubble_sink, bubble_void, z_cells, x_cells, y_cells)

    first = jnp.stack([cond_temp[0], cond_ion[0]])
    last = jnp.stack([cond_temp[-1], cond_ion[-1]])
    from_below = lax.ppermute(last, "gz", [(i, i + 1) for i in range(chain - 1)])
    from_above = lax.ppermute(first, "gz", [(i + 1, i) for i in range(chain - 1)])
    lo = jnp.where(position == 0, 2.0 * first, face(from_below, first))
    hi = jnp.where(position == chain - 1, 0.0, face(last, from_above))

    beta = jnp.where(position == 0, 0.0, lo)
    alpha = hi
    yt, yi, vt, vi, wt, wi, pack = local_solve(
        rhs_temp, rhs_ion, cond_temp, cond_ion, sources, lo, hi, beta
    )
    size = 4 if chain % 4 == 0 and chain > 4 else chain
    groups_z = chain // size
    member = position % size
    group = position // size
    zero = jnp.zeros_like(lo)

    members = gather_ring(pack, size, 1, member)
    packs, rights = [], []
    for r, m in enumerate(members):
        a, b, c, e, yf, yl = (m[j] for j in range(6))
        right_sets = [(yf, yl), (zero, zero), (zero, zero)]
        if r == 0:
            right_sets[1] = (-a, -c)
            a, c = zero, zero
        if r == size - 1:
            right_sets[2] = (-b, -e)
            b, e = zero, zero
        packs.append((a, b, c, e))
        rights.append(right_sets)
    firsts, lasts = chain_solve(packs, rights)
    if groups_z > 1:
        group_pack = jnp.stack([
            -firsts[0][1], -firsts[0][2], -lasts[-1][1], -lasts[-1][2], firsts[0][0], lasts[-1][0]
        ])
        tops = gather_ring(group_pack, groups_z, size, group)
        gpacks = [(t[0], t[1], t[2], t[3]) for t in tops]
        grights = [[(t[4], t[5])] for t in tops]
        gfirsts, glasts = chain_solve(gpacks, grights)
        outside_low = select([zero] + [l[0] for l in glasts[:-1]], group)
        outside_high = select([f[0] for f in gfirsts[1:]] + [zero], group)
    else:
        outside_low = zero
        outside_high = zero

    def value(parts):
        return parts[0] + outside_low * parts[1] + outside_high * parts[2]

    last_prev = select([outside_low] + [value(l) for l in lasts[:-1]], member)
    first_next = select([value(f) for f in firsts[1:]] + [outside_high], member)
    y = (yt, yi)
    v = (vt, vi)
    w = (wt, wi)
    outs = []
    for k in range(2):
        outs.append(
            y[k]
            + v[k] * (beta[k] * last_prev[k])[None]
            + w[k] * (alpha[k] * first_next[k])[None]
        )
    return tuple(outs)


def solution(mesh):
    in_specs = (
        P("gz", "gx", None),
        P("gz", "gx", None),
        P("gz", "gx", None),
        P("gz", "gx", None),
        P("gz", "gx"),
        P("gz", "gx", None),
        P("gz", "gx", None),
    )
    out_specs = (P("gz", "gx", None), P("gz", "gx", None))
    return jax.shard_map(body, mesh=mesh, in_specs=in_specs, out_specs=out_specs, check_vma=False)
```

```python
import functools

import jax
import jax.numpy as jnp
from jax import lax
from jax.experimental import pallas as pl
from jax.experimental.pallas import tpu as pltpu
from jax.sharding import PartitionSpec as P

ion_rate = 40.0
HIGH = lax.Precision.HIGH


def face(lower, upper):
    return 2.0 * lower * upper / (lower + upper)


CHUNKS = 4


def local_kernel(rt_hbm, ri_hbm, ct_hbm, ci_hbm, src_hbm, lo_ref, hi_ref, beta_ref,
                 yt_hbm, yi_hbm, vt_hbm, vi_hbm, wt_hbm, wi_hbm, pack_ref,
                 rt_ref, ri_ref, ct_ref, ci_ref, src_ref,
                 yt_ref, yi_ref, vt_ref, vi_ref, wt_ref, wi_ref, in_sem, out_sem):
    z_cells = rt_ref.shape[0]
    y_cells = rt_ref.shape[2]
    rows = z_cells // CHUNKS
    ins = ((rt_hbm, rt_ref), (ri_hbm, ri_ref), (src_hbm, src_ref), (ct_hbm, ct_ref), (ci_hbm, ci_ref))
    outs = ((yt_ref, yt_hbm), (yi_ref, yi_hbm), (vt_ref, vt_hbm), (vi_ref, vi_hbm), (wt_ref, wt_hbm), (wi_ref, wi_hbm))

    def copy_in(i, c):
        src_of, dst_of = ins[i]
        return pltpu.make_async_copy(
            src_of.at[pl.ds(c * rows, rows)], dst_of.at[pl.ds(c * rows, rows)], in_sem.at[i, c]
        )

    def copy_out(j, c):
        src_of, dst_of = outs[j]
        return pltpu.make_async_copy(
            src_of.at[pl.ds(c * rows, rows)], dst_of.at[pl.ds(c * rows, rows)], out_sem.at[j, c]
        )

    for c in range(CHUNKS):
        for i in (3, 4, 0, 1, 2):
            copy_in(i, c).start()

    cond_ready = set()

    def wait_chunk(c):
        for cc in (c, c + 1):
            if cc < CHUNKS and cc not in cond_ready:
                copy_in(3, cc).wait()
                copy_in(4, cc).wait()
                cond_ready.add(cc)
        for i in (0, 1, 2):
            copy_in(i, c).wait()

    fields = (
        (rt_ref, ct_ref, yt_ref, vt_ref, wt_ref, 0),
        (ri_ref, ci_ref, yi_ref, vi_ref, wi_ref, 1),
    )

    def absorb_of(k, z):
        part = src_ref[z, :, k * y_cells:(k + 1) * y_cells]
        return part if k == 0 else ion_rate * part

    wait_chunk(0)
    carry = []
    for rhs_ref, c_ref, y_ref, v_ref, w_ref, k in fields:
        below = lo_ref[k]
        above = face(c_ref[0], c_ref[1])
        main = 1.0 + below + above + absorb_of(k, 0)
        rp = 1.0 / main
        f = -above * rp
        dy = rhs_ref[0] * rp
        dv = rp
        w_ref[0] = f
        y_ref[0] = dy
        v_ref[0] = dv
        carry += [above, f, dy, dv]

    def fwd(z, carry):
        out = []
        for n, (rhs_ref, c_ref, y_ref, v_ref, w_ref, k) in enumerate(fields):
            below, f_prev, dy_prev, dv_prev = carry[4 * n:4 * n + 4]
            above = face(c_ref[z], c_ref[z + 1])
            main = 1.0 + below + above + absorb_of(k, z)
            pivot = main + below * f_prev
            rp = 1.0 / pivot
            f = -above * rp
            dy = (rhs_ref[z] + below * dy_prev) * rp
            dv = (below * dv_prev) * rp
            w_ref[z] = f
            y_ref[z] = dy
            v_ref[z] = dv
            out += [above, f, dy, dv]
        return tuple(out)

    carry = tuple(carry)
    for c in range(CHUNKS):
        if c > 0:
            wait_chunk(c)
        low = max(1, c * rows)
        high = min(z_cells - 1, (c + 1) * rows)
        carry = lax.fori_loop(low, high, fwd, carry, unroll=True)

    z = z_cells - 1
    back = []
    for n, (rhs_ref, c_ref, y_ref, v_ref, w_ref, k) in enumerate(fields):
        below, f_prev, dy_prev, dv_prev = carry[4 * n:4 * n + 4]
        above = hi_ref[k]
        main = 1.0 + below + above + absorb_of(k, z)
        pivot = main + below * f_prev
        rp = 1.0 / pivot
        dy = (rhs_ref[z] + below * dy_prev) * rp
        dv = (below * dv_prev) * rp
        y_ref[z] = dy
        v_ref[z] = dv
        w_ref[z] = rp
        back += [dy, dv, rp]

    def bwd(z, back):
        out = []
        for n, (rhs_ref, c_ref, y_ref, v_ref, w_ref, k) in enumerate(fields):
            y_next, v_next, w_next = back[3 * n:3 * n + 3]
            f = w_ref[z]
            y_val = y_ref[z] - f * y_next
            v_val = v_ref[z] - f * v_next
            w_val = -f * w_next
            y_ref[z] = y_val
            v_ref[z] = v_val
            w_ref[z] = w_val
            out += [y_val, v_val, w_val]
        return tuple(out)

    back = tuple(back)
    for c in reversed(range(CHUNKS)):
        low = c * rows
        high = min(z_cells - 1, (c + 1) * rows)
        back = lax.fori_loop(
            0, high - low, lambda i, b: bwd(high - 1 - i, b), back, unroll=True
        )
        for j in range(6):
            copy_out(j, c).start()
    for n, (rhs_ref, c_ref, y_ref, v_ref, w_ref, k) in enumerate(fields):
        y_first, v_first, w_first = back[3 * n:3 * n + 3]
        beta = beta_ref[k]
        alpha = hi_ref[k]
        pack_ref[0, k] = -v_first * beta
        pack_ref[1, k] = -w_first * alpha
        pack_ref[2, k] = -v_ref[z_cells - 1] * beta
        pack_ref[3, k] = -w_ref[z_cells - 1] * alpha
        pack_ref[4, k] = y_first
        pack_ref[5, k] = y_ref[z_cells - 1]
    for c in range(CHUNKS):
        for j in range(6):
            copy_out(j, c).wait()


def local_solve(rhs_temp, rhs_ion, cond_temp, cond_ion, sources, lo, hi, beta):
    shape = jax.ShapeDtypeStruct(rhs_temp.shape, jnp.float32)
    pack = jax.ShapeDtypeStruct((6,) + lo.shape, jnp.float32)
    vmem = pl.BlockSpec(memory_space=pltpu.VMEM)
    hbm = pl.BlockSpec(memory_space=pl.ANY)
    plane = pltpu.VMEM(rhs_temp.shape, jnp.float32)
    return pl.pallas_call(
        local_kernel,
        out_shape=(shape,) * 6 + (pack,),
        in_specs=[hbm] * 5 + [vmem] * 3,
        out_specs=(hbm,) * 6 + (vmem,),
        scratch_shapes=[plane] * 4
        + [pltpu.VMEM(sources.shape, jnp.float32)]
        + [plane] * 6
        + [pltpu.SemaphoreType.DMA((5, CHUNKS)), pltpu.SemaphoreType.DMA((6, CHUNKS))],
    )(rhs_temp, rhs_ion, cond_temp, cond_ion, sources, lo, hi, beta)


def chain_solve(packs, rights):
    count = len(packs)
    g1_prev = None
    zl_prev = None
    steps = []
    for i in range(count):
        a, b, c, e = packs[i]
        if g1_prev is None:
            z0 = [yf for yf, yl in rights[i]]
            zl = [yl for yf, yl in rights[i]]
            g0 = b
            g1 = e
        else:
            p = 1.0 - a * g1_prev
            rp = 1.0 / p
            g0 = b * rp
            t = c * g1_prev
            g1 = e + t * g0
            z0 = [(yf - a * zp) * rp for (yf, yl), zp in zip(rights[i], zl_prev)]
            zl = [yl - c * zp + t * z for (yf, yl), zp, z in zip(rights[i], zl_prev, z0)]
        steps.append((g0, g1, z0, zl))
        g1_prev, zl_prev = g1, zl
    firsts = [None] * count
    lasts = [None] * count
    f_next = None
    for i in reversed(range(count)):
        g0, g1, z0, zl = steps[i]
        if f_next is None:
            firsts[i], lasts[i] = z0, zl
        else:
            firsts[i] = [z - g0 * f for z, f in zip(z0, f_next)]
            lasts[i] = [z - g1 * f for z, f in zip(zl, f_next)]
        f_next = firsts[i]
    return firsts, lasts


def gather_ring(pack, size, stride, index):
    chain = lax.axis_size("gz")
    got = {0: pack}
    for s in range(1, size):
        route = []
        for i in range(chain):
            base = i - (i // stride % size) * stride
            route.append((i, base + ((i // stride + s) % size) * stride))
        got[s] = lax.ppermute(pack, "gz", route)
    ordered = []
    for member in range(size):
        pick = got[0]
        for s in range(1, size):
            pick = jnp.where((index - member) % size == s, got[s], pick)
        ordered.append(pick)
    return ordered


def select(values, index):
    out = jnp.zeros_like(values[0])
    for i, value in enumerate(values):
        out = jnp.where(index == i, value, out)
    return out


def deposit(bubble_target, bubble_sink, bubble_void, z_cells, x_cells, y_cells):
    cell_total = z_cells * x_cells
    groups = lax.axis_size("gx")
    target = bubble_target[0]
    record_total = target.shape[0]
    slot_count = 3 * record_total // groups
    width = 2 * y_cells
    payload = jnp.concatenate([bubble_sink[0], bubble_void[0]], axis=1)
    destination = target // cell_total
    cell_index = target % cell_total
    owners = lax.broadcasted_iota(jnp.int32, (record_total, groups), 1)
    owner_hot = (destination[:, None] == owners).astype(jnp.float32)
    row_ids = lax.broadcasted_iota(jnp.int32, (record_total, record_total), 0)
    col_ids = lax.broadcasted_iota(jnp.int32, (record_total, record_total), 1)
    earlier = (row_ids > col_ids).astype(jnp.float32)
    before = jnp.dot(earlier, owner_hot, precision=HIGH)
    rank_within = jnp.sum(before * owner_hot, axis=1).astype(jnp.int32)
    rows_per = slot_count + 1
    out_dest = lax.broadcasted_iota(jnp.int32, (groups, rows_per, record_total), 0)
    out_slot = lax.broadcasted_iota(jnp.int32, (groups, rows_per, record_total), 1)
    mine = destination[None, None, :] == out_dest
    pick = jnp.concatenate(
        [mine & (rank_within[None, None, :] == out_slot), mine & (out_slot == slot_count)], axis=2
    ).astype(jnp.float32)
    lanes = lax.broadcasted_iota(jnp.int32, (record_total, width), 1)
    cell_plus = (cell_index + 1).astype(jnp.float32)
    cell_lanes = jnp.where(lanes == rank_within[:, None], cell_plus[:, None], 0.0)
    stacked = jnp.concatenate([payload, cell_lanes], axis=0)
    send = jnp.einsum("dsr,rk->dsk", pick, stacked, precision=HIGH)
    received = lax.all_to_all(send, "gx", split_axis=0, concat_axis=0, tiled=True)
    rows = received[:, :slot_count, :].reshape(groups * slot_count, width)
    cells = received[:, slot_count, :slot_count].reshape(groups * slot_count) - 1.0
    cell_ids = lax.broadcasted_iota(jnp.int32, (cell_total, groups * slot_count), 0).astype(jnp.float32)
    spread = (cell_ids == cells[None, :]).astype(jnp.float32)
    sources = jnp.dot(spread, rows, precision=HIGH)
    return sources.reshape(z_cells, x_cells, width)


def body(rhs_temp, rhs_ion, cond_temp, cond_ion, bubble_target, bubble_sink, bubble_void):
    z_cells, x_cells, y_cells = rhs_temp.shape
    chain = lax.axis_size("gz")
    position = lax.axis_index("gz")
    sources = deposit(bubble_target, bubble_sink, bubble_void, z_cells, x_cells, y_cells)

    first = jnp.stack([cond_temp[0], cond_ion[0]])
    last = jnp.stack([cond_temp[-1], cond_ion[-1]])
    from_below = lax.ppermute(last, "gz", [(i, i + 1) for i in range(chain - 1)])
    from_above = lax.ppermute(first, "gz", [(i + 1, i) for i in range(chain - 1)])
    lo = jnp.where(position == 0, 2.0 * first, face(from_below, first))
    hi = jnp.where(position == chain - 1, 0.0, face(last, from_above))

    beta = jnp.where(position == 0, 0.0, lo)
    alpha = hi
    yt, yi, vt, vi, wt, wi, pack = local_solve(
        rhs_temp, rhs_ion, cond_temp, cond_ion, sources, lo, hi, beta
    )
    size = 4 if chain % 4 == 0 and chain > 4 else chain
    groups_z = chain // size
    member = position % size
    group = position // size
    zero = jnp.zeros_like(lo)

    members = gather_ring(pack, size, 1, member)
    packs, rights = [], []
    for r, m in enumerate(members):
        a, b, c, e, yf, yl = (m[j] for j in range(6))
        right_sets = [(yf, yl), (zero, zero), (zero, zero)]
        if r == 0:
            right_sets[1] = (-a, -c)
            a, c = zero, zero
        if r == size - 1:
            right_sets[2] = (-b, -e)
            b, e = zero, zero
        packs.append((a, b, c, e))
        rights.append(right_sets)
    firsts, lasts = chain_solve(packs, rights)
    if groups_z > 1:
        group_pack = jnp.stack([
            -firsts[0][1], -firsts[0][2], -lasts[-1][1], -lasts[-1][2], firsts[0][0], lasts[-1][0]
        ])
        tops = gather_ring(group_pack, groups_z, size, group)
        gpacks = [(t[0], t[1], t[2], t[3]) for t in tops]
        grights = [[(t[4], t[5])] for t in tops]
        gfirsts, glasts = chain_solve(gpacks, grights)
        outside_low = select([zero] + [l[0] for l in glasts[:-1]], group)
        outside_high = select([f[0] for f in gfirsts[1:]] + [zero], group)
    else:
        outside_low = zero
        outside_high = zero

    def value(parts):
        return parts[0] + outside_low * parts[1] + outside_high * parts[2]

    last_prev = select([outside_low] + [value(l) for l in lasts[:-1]], member)
    first_next = select([value(f) for f in firsts[1:]] + [outside_high], member)
    y = (yt, yi)
    v = (vt, vi)
    w = (wt, wi)
    outs = []
    for k in range(2):
        outs.append(
            y[k]
            + v[k] * (beta[k] * last_prev[k])[None]
            + w[k] * (alpha[k] * first_next[k])[None]
        )
    return tuple(outs)


def solution(mesh):
    in_specs = (
        P("gz", "gx", None),
        P("gz", "gx", None),
        P("gz", "gx", None),
        P("gz", "gx", None),
        P("gz", "gx"),
        P("gz", "gx", None),
        P("gz", "gx", None),
    )
    out_specs = (P("gz", "gx", None), P("gz", "gx", None))
    return jax.shard_map(body, mesh=mesh, in_specs=in_specs, out_specs=out_specs, check_vma=False)
```
